32 devices in a mesh: groups: 2 (over x), src: 16 (over z, y, core).
Axes of the slice: x: 2, y: 2, z: 4, core: 2. Of those that a mesh axis runs over, the one named last changes fastest.
Arguments:
- perambulator: bfloat16 [32, 5, 2, 512, 512], P(('groups', 'src')), parts along dimension 0, may hold values from -0.1875 to 0.1875
- source_meson: bfloat16 [32, 2, 128, 128], P(('groups', 'src')), parts along dimension 0, may hold values from -0.375 to 0.375
- sink_meson: bfloat16 [32, 2, 128, 128], P(('groups', 'src')), parts along dimension 0, may hold values from -0.375 to 0.375
- gamma_order: int32 [2, 4], replicated, may hold values from 0 to 3, each once within a row
- gamma_phase: int32 [2, 4], replicated, may hold values from 0 to 3
- diagram_blocks: int32 [2, 8192], P(None, 'src'), may hold values from 0 to 79
- diagram_codes: int32 [8192], P('src'), may hold values from 0 to 3
Outputs:
- box_traces: float32 [2, 16384], P(None, ('groups', 'src')), parts along dimension 1
The draws below stay inside these ranges and needn't reach their ends.
There are 2 independent parts, one for each index of `groups`. The reference program is written for one: setup_inputs(seed, part) draws one part's arguments, and reference() takes and returns one part's arrays. A program takes and returns all parts, laid end to end along the dimension named above; an argument that names none is the same for every part. Nothing has to cross between parts.
Inputs may be any that keep to these rules, and one draw needn't show every extreme that they name: `gamma_order`: each row is an ordering of the 4 spins.
All inputs are finite; a program needn't handle non-finite values.
Results may differ from the reference program's by a relative error of at most 0.0079.
Values may be sent and summed in bfloat16 or wider, within the bound.
No kernel may reach another device: no remote copies, remote signals or barrier semaphores. Data moves between devices by JAX's collectives and lax.ppermute only.
A program may use at most 192 MiB of HBM per device.

```python
import math
import jax
import jax.numpy as jnp
import numpy as np
from jax import lax

VECTORS = 128
SPINS = 4
ORDER = 512
REACH = 2
TIMES = 16
BLOCKS = 80
DIAGRAMS = 8192


def plant(entries, stream_key, smallest, largest):
    dims = entries.shape
    spot = [jax.random.randint(jax.random.fold_in(stream_key, axis), (), 0, dims[axis]) for axis in range(len(dims))]
    entries = entries.at[tuple(spot)].set(smallest)
    longest = dims.index(max(dims))
    spot[longest] = (spot[longest] + 1) % dims[longest]
    return entries.at[tuple(spot)].set(largest)


def shard_levels(stream_key, extent, shards, low, high):
    def one(dim, blocks):
        steps = jax.random.uniform(jax.random.fold_in(jax.random.fold_in(stream_key, 6), dim), (blocks,), jnp.float32, low / len(shards), high / len(shards))
        return jnp.repeat(jnp.exp(steps), extent[dim] // blocks).reshape((-1,) + (1,) * (len(extent) - dim - 1))

    level = one(*shards[0])
    for cut in shards[1:]:
        level = level * one(*cut)
    return level


def rank_table(count, skew):
    portions = [(1 << 20) // math.isqrt(rank ** skew) + 1 for rank in range(1, count + 1)]
    spread = 1 + sum(portions) // (1 << 30)
    return np.cumsum(np.array([max(1, weight // spread) for weight in portions]))


def ranked_ids(rng, dims, amount, skew):
    table = rank_table(amount, skew)
    lot = jax.random.randint(jax.random.fold_in(rng, 1), dims, 0, int(table[amount - 1]))
    rank = jnp.searchsorted(jnp.asarray(table, jnp.int32), lot, side="right")
    return jax.random.permutation(jax.random.fold_in(rng, 2), amount)[rank].astype(jnp.int32)


def noise(own_key, dims, spread, reach, split=(), kind=jnp.bfloat16):
    factor_of = shard_levels(own_key, dims, split, -0.22, 0.18) if split else 1.0
    array = jax.random.normal(own_key, dims, jnp.float32) * spread * factor_of
    return jnp.minimum(jnp.maximum(array, -reach), reach).astype(kind)


def setup_inputs(seed: int = 0, part: int = 0) -> dict:
    key_list = jax.random.split(jax.random.key(seed), 8)
    part_keys = jax.random.split(jax.random.fold_in(key_list[7], part), 8)
    perambulator = noise(part_keys[0], (TIMES, 2 * REACH + 1, 2, ORDER, ORDER), (2 * ORDER) ** -0.5, 0.1875, ((0, 16),))
    source_meson = noise(part_keys[1], (TIMES, 2, VECTORS, VECTORS), (2 * VECTORS) ** -0.5, 0.375, ((0, 16),))
    sink_meson = noise(part_keys[2], (TIMES, 2, VECTORS, VECTORS), (2 * VECTORS) ** -0.5, 0.375, ((0, 16),))
    gamma_order = jax.vmap(lambda own: jax.random.permutation(own, SPINS))(jax.random.split(key_list[3], 2)).reshape((2, SPINS)).astype(jnp.int32)
    gamma_phase = plant(jax.random.randint(key_list[4], (2, SPINS), 0, 4), jax.random.fold_in(key_list[4], 1), 0, 3).astype(jnp.int32)
    diagram_blocks = plant(ranked_ids(key_list[5], (2, DIAGRAMS), BLOCKS, 2), jax.random.fold_in(key_list[5], 3), 0, BLOCKS - 1).astype(jnp.int32)
    diagram_codes = plant(jax.random.randint(key_list[6], (DIAGRAMS,), 0, 4), jax.random.fold_in(key_list[6], 1), 0, 3).astype(jnp.int32)
    return {"perambulator": perambulator, "source_meson": source_meson, "sink_meson": sink_meson, "gamma_order": gamma_order, "gamma_phase": gamma_phase, "diagram_blocks": diagram_blocks, "diagram_codes": diagram_codes}


def apply_meson(elemental, order_row, phase_row, tile_pair):
    nvec = elemental.shape[-1]
    spin_count = tile_pair.shape[-1] // nvec
    split_tile = tile_pair.reshape(2, spin_count, nvec, tile_pair.shape[-1]).astype(jnp.float32)
    meson = elemental.astype(jnp.float32)

    def spin_mix(left, right):
        return jnp.einsum("ik,bkn->bin", left, right, precision=lax.Precision.HIGHEST)

    real_part = spin_mix(meson[0], split_tile[0]) - spin_mix(meson[1], split_tile[1])
    imag_part = spin_mix(meson[0], split_tile[1]) + spin_mix(meson[1], split_tile[0])
    chosen = (order_row[:, None] == jnp.arange(spin_count, dtype=jnp.int32)[None, :]).astype(jnp.float32)
    cosine = ((phase_row == 0).astype(jnp.float32) - (phase_row == 2).astype(jnp.float32))[:, None] * chosen
    sine_part = ((phase_row == 1).astype(jnp.float32) - (phase_row == 3).astype(jnp.float32))[:, None] * chosen

    def spin_pick(table, values):
        return jnp.einsum("ab,bin->ain", table, values, precision=lax.Precision.HIGHEST)

    mapped_re = spin_pick(cosine, real_part) - spin_pick(sine_part, imag_part)
    mapped_im = spin_pick(cosine, imag_part) + spin_pick(sine_part, real_part)
    result = jnp.stack([mapped_re, mapped_im]).reshape(2, spin_count * nvec, -1)
    return result.astype(jnp.bfloat16)


def complex_product(left, right):
    real_real = jnp.dot(left[0], right[0], preferred_element_type=jnp.float32)
    imag_imag = jnp.dot(left[1], right[1], preferred_element_type=jnp.float32)
    real_imag = jnp.dot(left[0], right[1], preferred_element_type=jnp.float32)
    imag_real = jnp.dot(left[1], right[0], preferred_element_type=jnp.float32)
    return jnp.stack([real_real - imag_imag, real_imag + imag_real]).astype(jnp.bfloat16)


def reference(perambulator, source_meson, sink_meson, gamma_order, gamma_phase, diagram_blocks, diagram_codes):
    window = 2 * REACH + 1

    def sink_side(inputs):
        meson, tiles = inputs
        return jnp.stack([apply_meson(meson, gamma_order[1], gamma_phase[1], tiles[position]) for position in range(window)])

    backward = lax.map(sink_side, (sink_meson, perambulator))

    def source_side(inputs):
        moment, meson, tiles = inputs
        loops = []
        for position in range(window):
            separation = position - REACH
            partner_time = ((moment + separation) % TIMES).astype(jnp.int32)
            partner_row = lax.dynamic_index_in_dim(backward, partner_time, 0, keepdims=False)
            forward = apply_meson(meson, gamma_order[0], gamma_phase[0], tiles[position])
            loops.append(complex_product(forward, partner_row[REACH - separation]))
        return jnp.stack(loops)

    open_loops = lax.map(source_side, (jnp.arange(TIMES, dtype=jnp.int32), source_meson, perambulator))
    flat_loops = open_loops.reshape(TIMES * window, 2, -1)
    real_flat = flat_loops[:, 0]
    imag_flat = flat_loops[:, 1]
    table_re = jnp.dot(real_flat, real_flat.T, preferred_element_type=jnp.float32) - jnp.dot(imag_flat, imag_flat.T, preferred_element_type=jnp.float32)
    table_im = jnp.dot(real_flat, imag_flat.T, preferred_element_type=jnp.float32) + jnp.dot(imag_flat, real_flat.T, preferred_element_type=jnp.float32)
    trace_table = jnp.stack([table_re, table_im])
    signs = 1 - 2 * (diagram_codes % 2)
    scales = 1 + diagram_codes // 2
    weight = (signs * scales).astype(jnp.float32)
    return trace_table[:, diagram_blocks[0], diagram_blocks[1]] * weight[None, :]
```

```python
import jax
import jax.numpy as jnp
from jax import lax
from jax.experimental import pallas as pl
from jax.experimental.pallas import tpu as pltpu
from jax.sharding import PartitionSpec as P


def shifted(block, axis, distance):
    devices = range(lax.axis_size(axis))
    route = [((i - distance) % len(devices), i) for i in devices]
    return lax.ppermute(block, axis, route)


def gamma_parts(order_row, phase_row):
    spins = order_row.shape[0]
    chosen = (order_row[:, None] == jnp.arange(spins, dtype=jnp.int32)[None, :]).astype(jnp.float32)
    cosine = ((phase_row == 0).astype(jnp.float32) - (phase_row == 2).astype(jnp.float32))[:, None] * chosen
    sine = ((phase_row == 1).astype(jnp.float32) - (phase_row == 3).astype(jnp.float32))[:, None] * chosen
    return cosine, sine


def dressing_matrix(elemental, order_row, phase_row):
    cosine, sine = gamma_parts(order_row, phase_row)
    meson = elemental.astype(jnp.float32)
    kron_re = jnp.kron(cosine, meson[0]) - jnp.kron(sine, meson[1])
    kron_im = jnp.kron(cosine, meson[1]) + jnp.kron(sine, meson[0])
    top = jnp.concatenate([kron_re, -kron_im], axis=1)
    bottom = jnp.concatenate([kron_im, kron_re], axis=1)
    return jnp.concatenate([top, bottom], axis=0).astype(jnp.bfloat16)


def dress(weights, tile_pair):
    order = tile_pair.shape[-1]
    stacked = tile_pair.reshape(2 * order, order)
    out = jnp.dot(weights, stacked, preferred_element_type=jnp.float32)
    return out.astype(jnp.bfloat16).reshape(2, order, order)


def loop_kernel(forward_ref, backward_ref, out_ref):
    fr = forward_ref[0, 0]
    fi = forward_ref[0, 1]
    br = backward_ref[0, 0]
    bi = backward_ref[0, 1]
    shares = out_ref.shape[0]
    rows = out_ref.shape[3]
    real = jnp.dot(fr, br, preferred_element_type=jnp.float32) - jnp.dot(fi, bi, preferred_element_type=jnp.float32)
    imag = jnp.dot(fr, bi, preferred_element_type=jnp.float32) + jnp.dot(fi, br, preferred_element_type=jnp.float32)
    out_ref[:, 0, 0] = real.astype(out_ref.dtype).reshape(shares, rows, real.shape[-1])
    out_ref[:, 0, 1] = imag.astype(out_ref.dtype).reshape(shares, rows, imag.shape[-1])


def open_loops(forward, backward, shares):
    window, _, order, _ = forward.shape
    rows = order // shares
    tile = pl.BlockSpec((1, 2, order, order), lambda s: (s, 0, 0, 0))
    return pl.pallas_call(
        loop_kernel,
        grid=(window,),
        in_specs=[tile, tile],
        out_specs=pl.BlockSpec((shares, 1, 2, rows, order), lambda s: (0, s, 0, 0, 0)),
        out_shape=jax.ShapeDtypeStruct((shares, window, 2, rows, order), jnp.bfloat16),
        compiler_params=pltpu.CompilerParams(vmem_limit_bytes=48 * 1024 * 1024),
        cost_estimate=pl.CostEstimate(
            flops=8 * window * order ** 3, transcendentals=0, bytes_accessed=6 * window * order * order * 2
        ),
    )(forward, backward)


def inner_product(left, right):
    return lax.dot_general(left, right, (((1,), (1,)), ((), ())), preferred_element_type=jnp.float32)


def all_sum(table, axis):
    n = lax.axis_size(axis)
    if n & (n - 1):
        return lax.psum(table, axis)
    bit = 1
    while bit < n:
        table = table + lax.ppermute(table, axis, [(i, i ^ bit) for i in range(n)])
        bit *= 2
    return table


def select_diagrams(trace_table, block_pairs, codes):
    signs = 1 - 2 * (codes % 2)
    scales = 1 + codes // 2
    weight = (signs * scales).astype(jnp.float32)
    return trace_table[:, block_pairs[0], block_pairs[1]] * weight[None, :]


def per_device(
    perambulator, source_meson, sink_meson, gamma_order, gamma_phase, diagram_blocks, diagram_codes
):
    window = perambulator.shape[1]
    half_window = window // 2
    shares = lax.axis_size("src")
    sink_weights = dressing_matrix(sink_meson[0], gamma_order[1], gamma_phase[1])
    backward = [dress(sink_weights, perambulator[0, position]) for position in range(window)]
    mirrored = {0: backward[half_window]}
    for offset in range(1, half_window + 1):
        for direction in (1, -1):
            separation = direction * offset
            mirrored[separation] = shifted(backward[half_window - separation], "src", -separation)
    source_weights = dressing_matrix(source_meson[0], gamma_order[0], gamma_phase[0])
    forward = jnp.stack([dress(source_weights, perambulator[0, position]) for position in range(window)])
    partners = jnp.stack([mirrored[position - half_window] for position in range(window)])
    loops = open_loops(forward, partners, shares)
    slices = lax.all_to_all(loops, "src", split_axis=0, concat_axis=0, tiled=True)
    block_count = slices.shape[0] * slices.shape[1]
    real_flat = slices[:, :, 0].reshape(block_count, -1)
    imag_flat = slices[:, :, 1].reshape(block_count, -1)
    trace_table = jnp.stack(
        [
            inner_product(real_flat, real_flat) - inner_product(imag_flat, imag_flat),
            inner_product(real_flat, imag_flat) + inner_product(imag_flat, real_flat),
        ]
    )
    summed = all_sum(trace_table, "src")
    return select_diagrams(summed, diagram_blocks, diagram_codes)


def solution(mesh):
    placed = (
        P(("groups", "src"), None, None, None, None),
        P(("groups", "src"), None, None, None),
        P(("groups", "src"), None, None, None),
        P(),
        P(),
        P(None, "src"),
        P("src"),
    )
    return jax.shard_map(
        per_device,
        mesh=mesh,
        in_specs=placed,
        out_specs=P(None, ("groups", "src")),
        check_vma=False,
    )
```

```python
import jax
import jax.numpy as jnp
from jax import lax
from jax.experimental import pallas as pl
from jax.experimental.pallas import tpu as pltpu
from jax.sharding import PartitionSpec as P


def shifted(block, axis, distance):
    devices = range(lax.axis_size(axis))
    route = [((i - distance) % len(devices), i) for i in devices]
    return lax.ppermute(block, axis, route)


def gamma_parts(order_row, phase_row):
    spins = order_row.shape[0]
    chosen = (order_row[:, None] == jnp.arange(spins, dtype=jnp.int32)[None, :]).astype(jnp.float32)
    cosine = ((phase_row == 0).astype(jnp.float32) - (phase_row == 2).astype(jnp.float32))[:, None] * chosen
    sine = ((phase_row == 1).astype(jnp.float32) - (phase_row == 3).astype(jnp.float32))[:, None] * chosen
    return cosine, sine


def dressing_matrix(elemental, order_row, phase_row):
    cosine, sine = gamma_parts(order_row, phase_row)
    meson = elemental.astype(jnp.float32)
    kron_re = jnp.kron(cosine, meson[0]) - jnp.kron(sine, meson[1])
    kron_im = jnp.kron(cosine, meson[1]) + jnp.kron(sine, meson[0])
    top = jnp.concatenate([kron_re, -kron_im], axis=1)
    bottom = jnp.concatenate([kron_im, kron_re], axis=1)
    return jnp.concatenate([top, bottom], axis=0).astype(jnp.bfloat16)


def dress(weights, tile_pair):
    order = tile_pair.shape[-1]
    stacked = tile_pair.reshape(2 * order, order)
    out = jnp.dot(weights, stacked, preferred_element_type=jnp.float32)
    return out.astype(jnp.bfloat16).reshape(2, order, order)


def loop_kernel(forward_ref, backward_ref, out_ref):
    fr = forward_ref[0, 0]
    fi = forward_ref[0, 1]
    br = backward_ref[0, 0]
    bi = backward_ref[0, 1]
    shares = out_ref.shape[0]
    rows = out_ref.shape[3]
    real = jnp.dot(fr, br, preferred_element_type=jnp.float32) - jnp.dot(fi, bi, preferred_element_type=jnp.float32)
    imag = jnp.dot(fr, bi, preferred_element_type=jnp.float32) + jnp.dot(fi, br, preferred_element_type=jnp.float32)
    out_ref[:, 0, 0] = real.astype(out_ref.dtype).reshape(shares, rows, real.shape[-1])
    out_ref[:, 0, 1] = imag.astype(out_ref.dtype).reshape(shares, rows, imag.shape[-1])


def open_loops(forward, backward, shares):
    window, _, order, _ = forward.shape
    rows = order // shares
    tile = pl.BlockSpec((1, 2, order, order), lambda s: (s, 0, 0, 0))
    return pl.pallas_call(
        loop_kernel,
        grid=(window,),
        in_specs=[tile, tile],
        out_specs=pl.BlockSpec((shares, 1, 2, rows, order), lambda s: (0, s, 0, 0, 0)),
        out_shape=jax.ShapeDtypeStruct((shares, window, 2, rows, order), jnp.bfloat16),
        compiler_params=pltpu.CompilerParams(vmem_limit_bytes=48 * 1024 * 1024),
        cost_estimate=pl.CostEstimate(
            flops=8 * window * order ** 3, transcendentals=0, bytes_accessed=6 * window * order * order * 2
        ),
    )(forward, backward)


def inner_product(left, right):
    return lax.dot_general(left, right, (((1,), (1,)), ((), ())), preferred_element_type=jnp.float32)


def all_sum(table, axis):
    n = lax.axis_size(axis)
    if n & (n - 1):
        return lax.psum(table, axis)
    bit = 1
    while bit < n:
        table = table + lax.ppermute(table, axis, [(i, i ^ bit) for i in range(n)])
        bit *= 2
    return table


def select_diagrams(trace_table, block_pairs, codes):
    signs = 1 - 2 * (codes % 2)
    scales = 1 + codes // 2
    weight = (signs * scales).astype(jnp.float32)
    return trace_table[:, block_pairs[0], block_pairs[1]] * weight[None, :]


def exchange_rows(loops, axis):
    n = lax.axis_size(axis)
    me = lax.axis_index(axis)
    pieces = [lax.dynamic_index_in_dim(loops, me, 0, keepdims=False)]
    for k in range(1, n):
        chunk = lax.dynamic_index_in_dim(loops, (me + k) % n, 0, keepdims=False)
        pieces.append(lax.ppermute(chunk, axis, [(i, (i + k) % n) for i in range(n)]))
    return jnp.stack(pieces)


def per_device(
    perambulator, source_meson, sink_meson, gamma_order, gamma_phase, diagram_blocks, diagram_codes
):
    window = perambulator.shape[1]
    half_window = window // 2
    shares = lax.axis_size("src")
    me = lax.axis_index("src")
    sink_weights = dressing_matrix(sink_meson[0], gamma_order[1], gamma_phase[1])
    backward = [dress(sink_weights, perambulator[0, position]) for position in range(window)]
    mirrored = {0: backward[half_window]}
    for offset in range(1, half_window + 1):
        for direction in (1, -1):
            separation = direction * offset
            mirrored[separation] = shifted(backward[half_window - separation], "src", -separation)
    source_weights = dressing_matrix(source_meson[0], gamma_order[0], gamma_phase[0])
    forward = [dress(source_weights, perambulator[0, position]) for position in range(window)]
    first = open_loops(forward[half_window][None], mirrored[0][None], shares)
    others = [position for position in range(window) if position != half_window]
    rest = open_loops(
        jnp.stack([forward[position] for position in others]),
        jnp.stack([mirrored[position - half_window] for position in others]),
        shares,
    )
    slices = jnp.concatenate([exchange_rows(first, "src"), exchange_rows(rest, "src")], axis=1)
    block_count = slices.shape[0] * slices.shape[1]
    real_flat = slices[:, :, 0].reshape(block_count, -1)
    imag_flat = slices[:, :, 1].reshape(block_count, -1)
    trace_table = jnp.stack(
        [
            inner_product(real_flat, real_flat) - inner_product(imag_flat, imag_flat),
            inner_product(real_flat, imag_flat) + inner_product(imag_flat, real_flat),
        ]
    )
    positions = [half_window] + others
    slot_of_position = [positions.index(position) for position in range(window)]
    block = jnp.arange(block_count, dtype=jnp.int32)
    source_time = block // window
    slot = jnp.asarray(slot_of_position, jnp.int32)[block % window]
    canonical = ((me - source_time) % shares) * window + slot
    trace_table = trace_table[:, canonical][:, :, canonical]
    summed = all_sum(trace_table, "src")
    return select_diagrams(summed, diagram_blocks, diagram_codes)


def solution(mesh):
    placed = (
        P(("groups", "src"), None, None, None, None),
        P(("groups", "src"), None, None, None),
        P(("groups", "src"), None, None, None),
        P(),
        P(),
        P(None, "src"),
        P("src"),
    )
    return jax.shard_map(
        per_device,
        mesh=mesh,
        in_specs=placed,
        out_specs=P(None, ("groups", "src")),
        check_vma=False,
    )
```

```python
import jax
import jax.numpy as jnp
from jax import lax
from jax.experimental import pallas as pl
from jax.experimental.pallas import tpu as pltpu
from jax.sharding import PartitionSpec as P


def shifted(block, axis, distance):
    devices = range(lax.axis_size(axis))
    route = [((i - distance) % len(devices), i) for i in devices]
    return lax.ppermute(block, axis, route)


def gamma_parts(order_row, phase_row):
    spins = order_row.shape[0]
    chosen = (order_row[:, None] == jnp.arange(spins, dtype=jnp.int32)[None, :]).astype(jnp.float32)
    cosine = ((phase_row == 0).astype(jnp.float32) - (phase_row == 2).astype(jnp.float32))[:, None] * chosen
    sine = ((phase_row == 1).astype(jnp.float32) - (phase_row == 3).astype(jnp.float32))[:, None] * chosen
    return cosine, sine


def dressing_matrix(elemental, order_row, phase_row):
    cosine, sine = gamma_parts(order_row, phase_row)
    meson = elemental.astype(jnp.float32)
    kron_re = jnp.kron(cosine, meson[0]) - jnp.kron(sine, meson[1])
    kron_im = jnp.kron(cosine, meson[1]) + jnp.kron(sine, meson[0])
    top = jnp.concatenate([kron_re, -kron_im], axis=1)
    bottom = jnp.concatenate([kron_im, kron_re], axis=1)
    return jnp.concatenate([top, bottom], axis=0).astype(jnp.bfloat16)


def dress(weights, tile_pair):
    order = tile_pair.shape[-1]
    stacked = tile_pair.reshape(2 * order, order)
    out = jnp.dot(weights, stacked, preferred_element_type=jnp.float32)
    return out.astype(jnp.bfloat16).reshape(2, order, order)


def loop_kernel(forward_ref, backward_ref, out_ref):
    fr = forward_ref[0, 0]
    fi = forward_ref[0, 1]
    br = backward_ref[0, 0]
    bi = backward_ref[0, 1]
    shares = out_ref.shape[0]
    rows = out_ref.shape[3]
    real = jnp.dot(fr, br, preferred_element_type=jnp.float32) - jnp.dot(fi, bi, preferred_element_type=jnp.float32)
    imag = jnp.dot(fr, bi, preferred_element_type=jnp.float32) + jnp.dot(fi, br, preferred_element_type=jnp.float32)
    out_ref[:, 0, 0] = real.astype(out_ref.dtype).reshape(shares, rows, real.shape[-1])
    out_ref[:, 0, 1] = imag.astype(out_ref.dtype).reshape(shares, rows, imag.shape[-1])


def open_loops(forward, backward, shares):
    window, _, order, _ = forward.shape
    rows = order // shares
    tile = pl.BlockSpec((1, 2, order, order), lambda s: (s, 0, 0, 0))
    return pl.pallas_call(
        loop_kernel,
        grid=(window,),
        in_specs=[tile, tile],
        out_specs=pl.BlockSpec((shares, 1, 2, rows, order), lambda s: (0, s, 0, 0, 0)),
        out_shape=jax.ShapeDtypeStruct((shares, window, 2, rows, order), jnp.bfloat16),
        compiler_params=pltpu.CompilerParams(vmem_limit_bytes=48 * 1024 * 1024),
        cost_estimate=pl.CostEstimate(
            flops=8 * window * order ** 3, transcendentals=0, bytes_accessed=6 * window * order * order * 2
        ),
    )(forward, backward)


def inner_product(left, right):
    return lax.dot_general(left, right, (((1,), (1,)), ((), ())), preferred_element_type=jnp.float32)


def all_sum(table, axis):
    n = lax.axis_size(axis)
    if n & (n - 1):
        return lax.psum(table, axis)
    bit = 1
    while bit < n:
        table = table + lax.ppermute(table, axis, [(i, i ^ bit) for i in range(n)])
        bit *= 2
    return table


def select_diagrams(trace_table, block_pairs, codes):
    signs = 1 - 2 * (codes % 2)
    scales = 1 + codes // 2
    weight = (signs * scales).astype(jnp.float32)
    return trace_table[:, block_pairs[0], block_pairs[1]] * weight[None, :]


def per_device(
    perambulator, source_meson, sink_meson, gamma_order, gamma_phase, diagram_blocks, diagram_codes
):
    window = perambulator.shape[1]
    half_window = window // 2
    shares = lax.axis_size("src")
    sink_weights = dressing_matrix(sink_meson[0], gamma_order[1], gamma_phase[1])
    backward = [dress(sink_weights, perambulator[0, position]) for position in range(window)]
    mirrored = {0: backward[half_window]}
    for offset in range(1, half_window + 1):
        for direction in (1, -1):
            separation = direction * offset
            mirrored[separation] = shifted(backward[half_window - separation], "src", -separation)
    source_weights = dressing_matrix(source_meson[0], gamma_order[0], gamma_phase[0])
    centre = open_loops(dress(source_weights, perambulator[0, half_window])[None], mirrored[0][None], shares)
    centre_slices = lax.all_to_all(centre, "src", split_axis=0, concat_axis=0, tiled=True)
    centre_slices, tiles = lax.optimization_barrier((centre_slices, perambulator[0]))
    others = [position for position in range(window) if position != half_window]
    rest = open_loops(
        jnp.stack([dress(source_weights, tiles[position]) for position in others]),
        jnp.stack([mirrored[position - half_window] for position in others]),
        shares,
    )
    rest_slices = lax.all_to_all(rest, "src", split_axis=0, concat_axis=0, tiled=True)
    slices = jnp.concatenate(
        [rest_slices[:, :half_window], centre_slices, rest_slices[:, half_window:]], axis=1
    )
    block_count = slices.shape[0] * slices.shape[1]
    real_flat = slices[:, :, 0].reshape(block_count, -1)
    imag_flat = slices[:, :, 1].reshape(block_count, -1)
    trace_table = jnp.stack(
        [
            inner_product(real_flat, real_flat) - inner_product(imag_flat, imag_flat),
            inner_product(real_flat, imag_flat) + inner_product(imag_flat, real_flat),
        ]
    )
    summed = all_sum(trace_table, "src")
    return select_diagrams(summed, diagram_blocks, diagram_codes)


def solution(mesh):
    placed = (
        P(("groups", "src"), None, None, None, None),
        P(("groups", "src"), None, None, None),
        P(("groups", "src"), None, None, None),
        P(),
        P(),
        P(None, "src"),
        P("src"),
    )
    return jax.shard_map(
        per_device,
        mesh=mesh,
        in_specs=placed,
        out_specs=P(None, ("groups", "src")),
        check_vma=False,
    )
```

```python
import jax
import jax.numpy as jnp
from jax import lax
from jax.experimental import pallas as pl
from jax.experimental.pallas import tpu as pltpu
from jax.sharding import PartitionSpec as P


def shifted(block, axis, distance):
    devices = range(lax.axis_size(axis))
    route = [((i - distance) % len(devices), i) for i in devices]
    return lax.ppermute(block, axis, route)


def gamma_parts(order_row, phase_row):
    spins = order_row.shape[0]
    chosen = (order_row[:, None] == jnp.arange(spins, dtype=jnp.int32)[None, :]).astype(jnp.float32)
    cosine = ((phase_row == 0).astype(jnp.float32) - (phase_row == 2).astype(jnp.float32))[:, None] * chosen
    sine = ((phase_row == 1).astype(jnp.float32) - (phase_row == 3).astype(jnp.float32))[:, None] * chosen
    return cosine, sine


def dressing_matrix(elemental, order_row, phase_row):
    cosine, sine = gamma_parts(order_row, phase_row)
    meson = elemental.astype(jnp.float32)
    kron_re = jnp.kron(cosine, meson[0]) - jnp.kron(sine, meson[1])
    kron_im = jnp.kron(cosine, meson[1]) + jnp.kron(sine, meson[0])
    top = jnp.concatenate([kron_re, -kron_im], axis=1)
    bottom = jnp.concatenate([kron_im, kron_re], axis=1)
    return jnp.concatenate([top, bottom], axis=0).astype(jnp.bfloat16)


def dress(weights, tile_pair):
    order = tile_pair.shape[-1]
    stacked = tile_pair.reshape(2 * order, order)
    out = jnp.dot(weights, stacked, preferred_element_type=jnp.float32)
    return out.astype(jnp.bfloat16).reshape(2, order, order)


def loop_kernel(forward_ref, backward_ref, out_ref):
    fr = forward_ref[0, 0]
    fi = forward_ref[0, 1]
    br = backward_ref[0, 0]
    bi = backward_ref[0, 1]
    shares = out_ref.shape[0]
    rows = out_ref.shape[3]
    real = jnp.dot(fr, br, preferred_element_type=jnp.float32) - jnp.dot(fi, bi, preferred_element_type=jnp.float32)
    imag = jnp.dot(fr, bi, preferred_element_type=jnp.float32) + jnp.dot(fi, br, preferred_element_type=jnp.float32)
    out_ref[:, 0, 0] = real.astype(out_ref.dtype).reshape(shares, rows, real.shape[-1])
    out_ref[:, 0, 1] = imag.astype(out_ref.dtype).reshape(shares, rows, imag.shape[-1])


def open_loops(forward, backward, shares):
    window, _, order, _ = forward.shape
    rows = order // shares
    tile = pl.BlockSpec((1, 2, order, order), lambda s: (s, 0, 0, 0))
    return pl.pallas_call(
        loop_kernel,
        grid=(window,),
        in_specs=[tile, tile],
        out_specs=pl.BlockSpec((shares, 1, 2, rows, order), lambda s: (0, s, 0, 0, 0)),
        out_shape=jax.ShapeDtypeStruct((shares, window, 2, rows, order), jnp.bfloat16),
        compiler_params=pltpu.CompilerParams(vmem_limit_bytes=48 * 1024 * 1024),
        cost_estimate=pl.CostEstimate(
            flops=8 * window * order ** 3, transcendentals=0, bytes_accessed=6 * window * order * order * 2
        ),
    )(forward, backward)


def rest_loop_kernel(*refs):
    forward_ref, partner_refs, out_ref = refs[0], refs[1:-1], refs[-1]
    step = pl.program_id(0)
    for index, partner_ref in enumerate(partner_refs):

        @pl.when(step == index)
        def _():
            loop_kernel(forward_ref, partner_ref, out_ref)


def rest_loops(forward, partners, shares):
    window, _, order, _ = forward.shape
    rows = order // shares
    tile = pl.BlockSpec((1, 2, order, order), lambda s: (s, 0, 0, 0))
    whole = pl.BlockSpec((1, 2, order, order), lambda s: (0, 0, 0, 0))
    return pl.pallas_call(
        rest_loop_kernel,
        grid=(window,),
        in_specs=[tile] + [whole] * len(partners),
        out_specs=pl.BlockSpec((shares, 1, 2, rows, order), lambda s: (0, s, 0, 0, 0)),
        out_shape=jax.ShapeDtypeStruct((shares, window, 2, rows, order), jnp.bfloat16),
        compiler_params=pltpu.CompilerParams(vmem_limit_bytes=48 * 1024 * 1024),
        cost_estimate=pl.CostEstimate(
            flops=8 * window * order ** 3, transcendentals=0, bytes_accessed=6 * window * order * order * 2
        ),
    )(forward, *[partner[None] for partner in partners])


def inner_product(left, right):
    return lax.dot_general(left, right, (((1,), (1,)), ((), ())), preferred_element_type=jnp.float32)


def all_sum(table, axis):
    n = lax.axis_size(axis)
    if n & (n - 1):
        return lax.psum(table, axis)
    stride = 1
    while stride < n:
        radix = 4 if n % (stride * 4) == 0 else 2
        received = [
            lax.ppermute(table, axis, [(i, i ^ (digit * stride)) for i in range(n)]) for digit in range(1, radix)
        ]
        for part in received:
            table = table + part
        stride *= radix
    return table


def select_diagrams(trace_table, block_pairs, codes):
    signs = 1 - 2 * (codes % 2)
    scales = 1 + codes // 2
    weight = (signs * scales).astype(jnp.float32)
    return trace_table[:, block_pairs[0], block_pairs[1]] * weight[None, :]


def per_device(
    perambulator, source_meson, sink_meson, gamma_order, gamma_phase, diagram_blocks, diagram_codes
):
    window = perambulator.shape[1]
    half_window = window // 2
    shares = lax.axis_size("src")
    sink_weights = dressing_matrix(sink_meson[0], gamma_order[1], gamma_phase[1])
    backward = [dress(sink_weights, perambulator[0, position]) for position in range(window)]
    source_weights = dressing_matrix(source_meson[0], gamma_order[0], gamma_phase[0])
    centre = open_loops(dress(source_weights, perambulator[0, half_window])[None], backward[half_window][None], shares)
    centre, backward = lax.optimization_barrier((centre, backward))
    mirrored = {0: backward[half_window]}
    for offset in range(1, half_window + 1):
        for direction in (1, -1):
            separation = direction * offset
            mirrored[separation] = shifted(backward[half_window - separation], "src", -separation)
    centre_slices = lax.all_to_all(centre, "src", split_axis=0, concat_axis=0, tiled=True)
    centre_slices, mirrored = lax.optimization_barrier((centre_slices, mirrored))
    others = [position for position in range(window) if position != half_window]
    rest = rest_loops(
        jnp.stack([dress(source_weights, perambulator[0, position]) for position in others]),
        [mirrored[position - half_window] for position in others],
        shares,
    )
    rest_slices = lax.all_to_all(rest, "src", split_axis=0, concat_axis=0, tiled=True)
    slices = jnp.concatenate(
        [rest_slices[:, :half_window], centre_slices, rest_slices[:, half_window:]], axis=1
    )
    block_count = slices.shape[0] * slices.shape[1]
    real_flat = slices[:, :, 0].reshape(block_count, -1)
    imag_flat = slices[:, :, 1].reshape(block_count, -1)
    trace_table = jnp.stack(
        [
            inner_product(real_flat, real_flat) - inner_product(imag_flat, imag_flat),
            inner_product(real_flat, imag_flat) + inner_product(imag_flat, real_flat),
        ]
    )
    summed = all_sum(trace_table, "src")
    return select_diagrams(summed, diagram_blocks, diagram_codes)


def solution(mesh):
    placed = (
        P(("groups", "src"), None, None, None, None),
        P(("groups", "src"), None, None, None),
        P(("groups", "src"), None, None, None),
        P(),
        P(),
        P(None, "src"),
        P("src"),
    )
    return jax.shard_map(
        per_device,
        mesh=mesh,
        in_specs=placed,
        out_specs=P(None, ("groups", "src")),
        check_vma=False,
    )
```

```python
import jax
import numpy as np
import jax.numpy as jnp
from jax import lax
from jax.experimental import pallas as pl
from jax.experimental.pallas import tpu as pltpu
from jax.sharding import PartitionSpec as P


def shifted(block, axis, distance):
    devices = range(lax.axis_size(axis))
    route = [((i - distance) % len(devices), i) for i in devices]
    return lax.ppermute(block, axis, route)


def gamma_parts(order_row, phase_row):
    spins = order_row.shape[0]
    chosen = (order_row[:, None] == jnp.arange(spins, dtype=jnp.int32)[None, :]).astype(jnp.float32)
    cosine = ((phase_row == 0).astype(jnp.float32) - (phase_row == 2).astype(jnp.float32))[:, None] * chosen
    sine = ((phase_row == 1).astype(jnp.float32) - (phase_row == 3).astype(jnp.float32))[:, None] * chosen
    return cosine, sine


def dressing_matrix(elemental, order_row, phase_row):
    cosine, sine = gamma_parts(order_row, phase_row)
    real, imag = elemental[0].astype(jnp.float32), elemental[1].astype(jnp.float32)
    plain = jnp.stack([jnp.stack([real, -imag], 1), jnp.stack([imag, real], 1)], 0)
    turned = jnp.stack([jnp.stack([-imag, -real], 1), jnp.stack([real, -imag], 1)], 0)
    spins = cosine.shape[0]
    weights = (
        cosine[None, :, None, None, :, None] * plain[:, None, :, :, None, :]
        + sine[None, :, None, None, :, None] * turned[:, None, :, :, None, :]
    )
    size = 2 * spins * real.shape[0]
    return weights.reshape(size, size).astype(jnp.bfloat16)


def dress(weights, tile_pair):
    order = tile_pair.shape[-1]
    stacked = tile_pair.reshape(2 * order, order)
    out = jnp.dot(weights, stacked, preferred_element_type=jnp.float32)
    return out.astype(jnp.bfloat16).reshape(2, order, order)


def loop_kernel(forward_ref, backward_ref, out_ref):
    fr = forward_ref[0, 0]
    fi = forward_ref[0, 1]
    br = backward_ref[0, 0]
    bi = backward_ref[0, 1]
    shares = out_ref.shape[0]
    rows = out_ref.shape[3]
    real = jnp.dot(fr, br, preferred_element_type=jnp.float32) - jnp.dot(fi, bi, preferred_element_type=jnp.float32)
    imag = jnp.dot(fr, bi, preferred_element_type=jnp.float32) + jnp.dot(fi, br, preferred_element_type=jnp.float32)
    out_ref[:, 0, 0] = real.astype(out_ref.dtype).reshape(shares, rows, real.shape[-1])
    out_ref[:, 0, 1] = imag.astype(out_ref.dtype).reshape(shares, rows, imag.shape[-1])


def open_loops(forward, backward, shares):
    window, _, order, _ = forward.shape
    rows = order // shares
    tile = pl.BlockSpec((1, 2, order, order), lambda s: (s, 0, 0, 0))
    return pl.pallas_call(
        loop_kernel,
        grid=(window,),
        in_specs=[tile, tile],
        out_specs=pl.BlockSpec((shares, 1, 2, rows, order), lambda s: (0, s, 0, 0, 0)),
        out_shape=jax.ShapeDtypeStruct((shares, window, 2, rows, order), jnp.bfloat16),
        compiler_params=pltpu.CompilerParams(vmem_limit_bytes=48 * 1024 * 1024),
        cost_estimate=pl.CostEstimate(
            flops=8 * window * order ** 3, transcendentals=0, bytes_accessed=6 * window * order * order * 2
        ),
    )(forward, backward)


def rest_loop_kernel(*refs):
    count = (len(refs) - 1) // 2
    forward_refs, partner_refs, out_ref = refs[:count], refs[count:-1], refs[-1]
    step = pl.program_id(0)
    for index in range(count):

        @pl.when(step == index)
        def _():
            loop_kernel(forward_refs[index], partner_refs[index], out_ref)


def rest_loops(forwards, partners, shares):
    count = len(forwards)
    _, order, _ = forwards[0].shape
    rows = order // shares
    whole = pl.BlockSpec((1, 2, order, order), lambda s: (0, 0, 0, 0))
    return pl.pallas_call(
        rest_loop_kernel,
        grid=(count,),
        in_specs=[whole] * (2 * count),
        out_specs=pl.BlockSpec((shares, 1, 2, rows, order), lambda s: (0, s, 0, 0, 0)),
        out_shape=jax.ShapeDtypeStruct((shares, count, 2, rows, order), jnp.bfloat16),
        compiler_params=pltpu.CompilerParams(vmem_limit_bytes=56 * 1024 * 1024),
        cost_estimate=pl.CostEstimate(
            flops=8 * count * order ** 3, transcendentals=0, bytes_accessed=6 * count * order * order * 2
        ),
    )(*[tile[None] for tile in forwards], *[tile[None] for tile in partners])


def inner_product(left, right):
    return lax.dot_general(left, right, (((1,), (1,)), ((), ())), preferred_element_type=jnp.float32)


def all_sum(table, axis):
    n = lax.axis_size(axis)
    if n & (n - 1):
        return lax.psum(table, axis)
    stride = 1
    while stride < n:
        radix = 4 if n % (stride * 4) == 0 else 2
        received = [
            lax.ppermute(table, axis, [(i, i ^ (digit * stride)) for i in range(n)]) for digit in range(1, radix)
        ]
        for part in received:
            table = table + part
        stride *= radix
    return table


def select_diagrams(trace_table, block_pairs, codes):
    signs = 1 - 2 * (codes % 2)
    scales = 1 + codes // 2
    weight = (signs * scales).astype(jnp.float32)
    return trace_table[:, block_pairs[0], block_pairs[1]] * weight[None, :]


def per_device(
    perambulator, source_meson, sink_meson, gamma_order, gamma_phase, diagram_blocks, diagram_codes
):
    window = perambulator.shape[1]
    half_window = window // 2
    shares = lax.axis_size("src")
    tiles = perambulator[0]
    mesons = jnp.stack([source_meson[0], sink_meson[0]])
    received = {}
    for offset in range(1, half_window + 1):
        received[offset] = (
            shifted(tiles[half_window - offset], "src", -offset),
            shifted(mesons, "src", -offset),
        )
    source_own = dressing_matrix(mesons[0], gamma_order[0], gamma_phase[0])
    sink_own = dressing_matrix(mesons[1], gamma_order[1], gamma_phase[1])
    centre = open_loops(
        dress(source_own, tiles[half_window])[None], dress(sink_own, tiles[half_window])[None], shares
    )
    centre_slices = lax.all_to_all(centre, "src", split_axis=0, concat_axis=0, tiled=True)
    forwards, partners = [], []
    own_forward = {offset: dress(source_own, tiles[half_window + offset]) for offset in received}
    own_backward = {offset: dress(sink_own, tiles[half_window + offset]) for offset in received}
    centre_slices, received = lax.optimization_barrier((centre_slices, received))
    for offset, (tile, partner_mesons) in received.items():
        source_partner = dressing_matrix(partner_mesons[0], gamma_order[0], gamma_phase[0])
        sink_partner = dressing_matrix(partner_mesons[1], gamma_order[1], gamma_phase[1])
        forwards += [own_forward[offset], dress(source_partner, tile)]
        partners += [dress(sink_partner, tile), own_backward[offset]]
    rest = rest_loops(forwards, partners, shares)
    rest_slices = lax.all_to_all(rest, "src", split_axis=0, concat_axis=0, tiled=True)
    slices = jnp.concatenate([centre_slices, rest_slices], axis=1)
    block_count = slices.shape[0] * slices.shape[1]
    real_flat = slices[:, :, 0].reshape(block_count, -1)
    imag_flat = slices[:, :, 1].reshape(block_count, -1)
    trace_table = jnp.stack(
        [
            inner_product(real_flat, real_flat) - inner_product(imag_flat, imag_flat),
            inner_product(real_flat, imag_flat) + inner_product(imag_flat, real_flat),
        ]
    )
    place = np.zeros(block_count, np.int32)
    for source in range(shares):
        place[source * window + half_window] = source * window
        for offset in range(1, half_window + 1):
            place[source * window + half_window + offset] = source * window + 2 * offset - 1
            place[((source + offset) % shares) * window + half_window - offset] = source * window + 2 * offset
    canonical = jnp.asarray(place)
    trace_table = trace_table[:, canonical][:, :, canonical]
    summed = all_sum(trace_table, "src")
    return select_diagrams(summed, diagram_blocks, diagram_codes)


def solution(mesh):
    placed = (
        P(("groups", "src"), None, None, None, None),
        P(("groups", "src"), None, None, None),
        P(("groups", "src"), None, None, None),
        P(),
        P(),
        P(None, "src"),
        P("src"),
    )
    return jax.shard_map(
        per_device,
        mesh=mesh,
        in_specs=placed,
        out_specs=P(None, ("groups", "src")),
        check_vma=False,
    )
```

```python
import jax
import numpy as np
import jax.numpy as jnp
from jax import lax
from jax.experimental import pallas as pl
from jax.experimental.pallas import tpu as pltpu
from jax.sharding import PartitionSpec as P


def shifted(block, axis, distance):
    devices = range(lax.axis_size(axis))
    route = [((i - distance) % len(devices), i) for i in devices]
    return lax.ppermute(block, axis, route)


def gamma_parts(order_row, phase_row):
    spins = order_row.shape[0]
    chosen = (order_row[:, None] == jnp.arange(spins, dtype=jnp.int32)[None, :]).astype(jnp.float32)
    cosine = ((phase_row == 0).astype(jnp.float32) - (phase_row == 2).astype(jnp.float32))[:, None] * chosen
    sine = ((phase_row == 1).astype(jnp.float32) - (phase_row == 3).astype(jnp.float32))[:, None] * chosen
    return cosine, sine


def dressing_matrix(elemental, order_row, phase_row):
    cosine, sine = gamma_parts(order_row, phase_row)
    meson = elemental.astype(jnp.float32)
    kron_re = jnp.kron(cosine, meson[0]) - jnp.kron(sine, meson[1])
    kron_im = jnp.kron(cosine, meson[1]) + jnp.kron(sine, meson[0])
    top = jnp.concatenate([kron_re, -kron_im], axis=1)
    bottom = jnp.concatenate([kron_im, kron_re], axis=1)
    return jnp.concatenate([top, bottom], axis=0).astype(jnp.bfloat16)


def dress(weights, tile_pair):
    order = tile_pair.shape[-1]
    stacked = tile_pair.reshape(2 * order, order)
    out = jnp.dot(weights, stacked, preferred_element_type=jnp.float32)
    return out.astype(jnp.bfloat16).reshape(2, order, order)


def loop_kernel(forward_ref, backward_ref, out_ref):
    fr = forward_ref[0, 0]
    fi = forward_ref[0, 1]
    br = backward_ref[0, 0]
    bi = backward_ref[0, 1]
    shares = out_ref.shape[0]
    rows = out_ref.shape[3]
    real = jnp.dot(fr, br, preferred_element_type=jnp.float32) - jnp.dot(fi, bi, preferred_element_type=jnp.float32)
    imag = jnp.dot(fr, bi, preferred_element_type=jnp.float32) + jnp.dot(fi, br, preferred_element_type=jnp.float32)
    out_ref[:, 0, 0] = real.astype(out_ref.dtype).reshape(shares, rows, real.shape[-1])
    out_ref[:, 0, 1] = imag.astype(out_ref.dtype).reshape(shares, rows, imag.shape[-1])


def open_loops(forward, backward, shares):
    window, _, order, _ = forward.shape
    rows = order // shares
    tile = pl.BlockSpec((1, 2, order, order), lambda s: (s, 0, 0, 0))
    return pl.pallas_call(
        loop_kernel,
        grid=(window,),
        in_specs=[tile, tile],
        out_specs=pl.BlockSpec((shares, 1, 2, rows, order), lambda s: (0, s, 0, 0, 0)),
        out_shape=jax.ShapeDtypeStruct((shares, window, 2, rows, order), jnp.bfloat16),
        compiler_params=pltpu.CompilerParams(vmem_limit_bytes=48 * 1024 * 1024),
        cost_estimate=pl.CostEstimate(
            flops=8 * window * order ** 3, transcendentals=0, bytes_accessed=6 * window * order * order * 2
        ),
    )(forward, backward)


def rest_loop_kernel(*refs):
    count = (len(refs) - 1) // 2
    forward_refs, partner_refs, out_ref = refs[:count], refs[count:-1], refs[-1]
    step = pl.program_id(0)
    for index in range(count):

        @pl.when(step == index)
        def _():
            loop_kernel(forward_refs[index], partner_refs[index], out_ref)


def rest_loops(forwards, partners, shares):
    count = len(forwards)
    _, order, _ = forwards[0].shape
    rows = order // shares
    whole = pl.BlockSpec((1, 2, order, order), lambda s: (0, 0, 0, 0))
    return pl.pallas_call(
        rest_loop_kernel,
        grid=(count,),
        in_specs=[whole] * (2 * count),
        out_specs=pl.BlockSpec((shares, 1, 2, rows, order), lambda s: (0, s, 0, 0, 0)),
        out_shape=jax.ShapeDtypeStruct((shares, count, 2, rows, order), jnp.bfloat16),
        compiler_params=pltpu.CompilerParams(vmem_limit_bytes=56 * 1024 * 1024),
        cost_estimate=pl.CostEstimate(
            flops=8 * count * order ** 3, transcendentals=0, bytes_accessed=6 * count * order * order * 2
        ),
    )(*[tile[None] for tile in forwards], *[tile[None] for tile in partners])


def inner_product(left, right):
    return lax.dot_general(left, right, (((1,), (1,)), ((), ())), preferred_element_type=jnp.float32)


def all_sum(table, axis):
    n = lax.axis_size(axis)
    if n & (n - 1):
        return lax.psum(table, axis)
    stride = 1
    while stride < n:
        radix = 4 if n % (stride * 4) == 0 else 2
        received = [
            lax.ppermute(table, axis, [(i, i ^ (digit * stride)) for i in range(n)]) for digit in range(1, radix)
        ]
        for part in received:
            table = table + part
        stride *= radix
    return table


def select_diagrams(trace_table, block_pairs, codes):
    signs = 1 - 2 * (codes % 2)
    scales = 1 + codes // 2
    weight = (signs * scales).astype(jnp.float32)
    return trace_table[:, block_pairs[0], block_pairs[1]] * weight[None, :]


def per_device(
    perambulator, source_meson, sink_meson, gamma_order, gamma_phase, diagram_blocks, diagram_codes
):
    window = perambulator.shape[1]
    half_window = window // 2
    shares = lax.axis_size("src")
    tiles = perambulator[0]
    mesons = jnp.stack([source_meson[0], sink_meson[0]])
    received = {}
    for offset in range(1, half_window + 1):
        received[offset] = (
            shifted(tiles[half_window - offset], "src", -offset),
            shifted(mesons, "src", -offset),
        )
    source_own = dressing_matrix(mesons[0], gamma_order[0], gamma_phase[0])
    sink_own = dressing_matrix(mesons[1], gamma_order[1], gamma_phase[1])
    centre = open_loops(
        dress(source_own, tiles[half_window])[None], dress(sink_own, tiles[half_window])[None], shares
    )
    centre_slices = lax.all_to_all(centre, "src", split_axis=0, concat_axis=0, tiled=True)
    forwards, partners = [], []
    own_forward = {offset: dress(source_own, tiles[half_window + offset]) for offset in received}
    own_backward = {offset: dress(sink_own, tiles[half_window + offset]) for offset in received}
    partner_weights = {
        offset: (
            dressing_matrix(partner_mesons[0], gamma_order[0], gamma_phase[0]),
            dressing_matrix(partner_mesons[1], gamma_order[1], gamma_phase[1]),
        )
        for offset, (_, partner_mesons) in received.items()
    }
    centre_slices, partner_tiles = lax.optimization_barrier(
        (centre_slices, {offset: tile for offset, (tile, _) in received.items()})
    )
    for offset, tile in partner_tiles.items():
        source_partner, sink_partner = partner_weights[offset]
        forwards += [own_forward[offset], dress(source_partner, tile)]
        partners += [dress(sink_partner, tile), own_backward[offset]]
    rest = rest_loops(forwards, partners, shares)
    rest_slices = lax.all_to_all(rest, "src", split_axis=0, concat_axis=0, tiled=True)
    slices = jnp.concatenate([centre_slices, rest_slices], axis=1)
    block_count = slices.shape[0] * slices.shape[1]
    real_flat = slices[:, :, 0].reshape(block_count, -1)
    imag_flat = slices[:, :, 1].reshape(block_count, -1)
    trace_table = jnp.stack(
        [
            inner_product(real_flat, real_flat) - inner_product(imag_flat, imag_flat),
            inner_product(real_flat, imag_flat) + inner_product(imag_flat, real_flat),
        ]
    )
    place = np.zeros(block_count, np.int32)
    for source in range(shares):
        place[source * window + half_window] = source * window
        for offset in range(1, half_window + 1):
            place[source * window + half_window + offset] = source * window + 2 * offset - 1
            place[((source + offset) % shares) * window + half_window - offset] = source * window + 2 * offset
    canonical = jnp.asarray(place)
    trace_table = trace_table[:, canonical][:, :, canonical]
    summed = all_sum(trace_table, "src")
    return select_diagrams(summed, diagram_blocks, diagram_codes)


def solution(mesh):
    placed = (
        P(("groups", "src"), None, None, None, None),
        P(("groups", "src"), None, None, None),
        P(("groups", "src"), None, None, None),
        P(),
        P(),
        P(None, "src"),
        P("src"),
    )
    return jax.shard_map(
        per_device,
        mesh=mesh,
        in_specs=placed,
        out_specs=P(None, ("groups", "src")),
        check_vma=False,
    )
```

```python
import jax
import numpy as np
import jax.numpy as jnp
from jax import lax
from jax.experimental import pallas as pl
from jax.experimental.pallas import tpu as pltpu
from jax.sharding import PartitionSpec as P


def shifted(block, axis, distance):
    devices = range(lax.axis_size(axis))
    route = [((i - distance) % len(devices), i) for i in devices]
    return lax.ppermute(block, axis, route)


def gamma_parts(order_row, phase_row):
    spins = order_row.shape[0]
    chosen = (order_row[:, None] == jnp.arange(spins, dtype=jnp.int32)[None, :]).astype(jnp.float32)
    cosine = ((phase_row == 0).astype(jnp.float32) - (phase_row == 2).astype(jnp.float32))[:, None] * chosen
    sine = ((phase_row == 1).astype(jnp.float32) - (phase_row == 3).astype(jnp.float32))[:, None] * chosen
    return cosine, sine


def dressing_matrix(elemental, order_row, phase_row):
    cosine, sine = gamma_parts(order_row, phase_row)
    meson = elemental.astype(jnp.float32)
    kron_re = jnp.kron(cosine, meson[0]) - jnp.kron(sine, meson[1])
    kron_im = jnp.kron(cosine, meson[1]) + jnp.kron(sine, meson[0])
    top = jnp.concatenate([kron_re, -kron_im], axis=1)
    bottom = jnp.concatenate([kron_im, kron_re], axis=1)
    return jnp.concatenate([top, bottom], axis=0).astype(jnp.bfloat16)


def dress(weights, tile_pair):
    order = tile_pair.shape[-1]
    stacked = tile_pair.reshape(2 * order, order)
    out = jnp.dot(weights, stacked, preferred_element_type=jnp.float32)
    return out.astype(jnp.bfloat16).reshape(2, order, order)


def loop_kernel(forward_ref, backward_ref, out_ref):
    fr = forward_ref[0, 0]
    fi = forward_ref[0, 1]
    br = backward_ref[0, 0]
    bi = backward_ref[0, 1]
    shares = out_ref.shape[0]
    rows = out_ref.shape[3]
    real = jnp.dot(fr, br, preferred_element_type=jnp.float32) - jnp.dot(fi, bi, preferred_element_type=jnp.float32)
    imag = jnp.dot(fr, bi, preferred_element_type=jnp.float32) + jnp.dot(fi, br, preferred_element_type=jnp.float32)
    out_ref[:, 0, 0] = real.astype(out_ref.dtype).reshape(shares, rows, real.shape[-1])
    out_ref[:, 0, 1] = imag.astype(out_ref.dtype).reshape(shares, rows, imag.shape[-1])


def open_loops(forward, backward, shares):
    window, _, order, _ = forward.shape
    rows = order // shares
    tile = pl.BlockSpec((1, 2, order, order), lambda s: (s, 0, 0, 0))
    return pl.pallas_call(
        loop_kernel,
        grid=(window,),
        in_specs=[tile, tile],
        out_specs=pl.BlockSpec((shares, 1, 2, rows, order), lambda s: (0, s, 0, 0, 0)),
        out_shape=jax.ShapeDtypeStruct((shares, window, 2, rows, order), jnp.bfloat16),
        compiler_params=pltpu.CompilerParams(vmem_limit_bytes=48 * 1024 * 1024),
        cost_estimate=pl.CostEstimate(
            flops=8 * window * order ** 3, transcendentals=0, bytes_accessed=6 * window * order * order * 2
        ),
    )(forward, backward)


def rest_loop_kernel(*refs):
    count = (len(refs) - 1) // 2
    forward_refs, partner_refs, out_ref = refs[:count], refs[count:-1], refs[-1]
    step = pl.program_id(0)
    for index in range(count):

        @pl.when(step == index)
        def _():
            loop_kernel(forward_refs[index], partner_refs[index], out_ref)


def rest_loops(forwards, partners, shares):
    count = len(forwards)
    _, order, _ = forwards[0].shape
    rows = order // shares
    whole = pl.BlockSpec((1, 2, order, order), lambda s: (0, 0, 0, 0))
    return pl.pallas_call(
        rest_loop_kernel,
        grid=(count,),
        in_specs=[whole] * (2 * count),
        out_specs=pl.BlockSpec((shares, 1, 2, rows, order), lambda s: (0, s, 0, 0, 0)),
        out_shape=jax.ShapeDtypeStruct((shares, count, 2, rows, order), jnp.bfloat16),
        compiler_params=pltpu.CompilerParams(vmem_limit_bytes=56 * 1024 * 1024),
        cost_estimate=pl.CostEstimate(
            flops=8 * count * order ** 3, transcendentals=0, bytes_accessed=6 * count * order * order * 2
        ),
    )(*[tile[None] for tile in forwards], *[tile[None] for tile in partners])


def inner_product(left, right):
    return lax.dot_general(left, right, (((1,), (1,)), ((), ())), preferred_element_type=jnp.float32)


def all_sum(table, axis):
    n = lax.axis_size(axis)
    if n & (n - 1):
        return lax.psum(table, axis)
    bit = 1
    while bit < n:
        table = table + lax.ppermute(table, axis, [(i, i ^ bit) for i in range(n)])
        bit *= 2
    return table


def select_diagrams(trace_table, block_pairs, codes):
    signs = 1 - 2 * (codes % 2)
    scales = 1 + codes // 2
    weight = (signs * scales).astype(jnp.float32)
    return trace_table[:, block_pairs[0], block_pairs[1]] * weight[None, :]


def per_device(
    perambulator, source_meson, sink_meson, gamma_order, gamma_phase, diagram_blocks, diagram_codes
):
    window = perambulator.shape[1]
    half_window = window // 2
    shares = lax.axis_size("src")
    tiles = perambulator[0]
    mesons = jnp.stack([source_meson[0], sink_meson[0]])
    received = {}
    for offset in range(1, half_window + 1):
        received[offset] = (
            shifted(tiles[half_window - offset], "src", -offset),
            shifted(mesons, "src", -offset),
        )
    source_own = dressing_matrix(mesons[0], gamma_order[0], gamma_phase[0])
    sink_own = dressing_matrix(mesons[1], gamma_order[1], gamma_phase[1])
    centre = open_loops(
        dress(source_own, tiles[half_window])[None], dress(sink_own, tiles[half_window])[None], shares
    )
    centre_slices = lax.all_to_all(centre, "src", split_axis=0, concat_axis=0, tiled=True)
    forwards, partners = [], []
    own_forward = {offset: dress(source_own, tiles[half_window + offset]) for offset in received}
    own_backward = {offset: dress(sink_own, tiles[half_window + offset]) for offset in received}
    partner_weights = {
        offset: (
            dressing_matrix(partner_mesons[0], gamma_order[0], gamma_phase[0]),
            dressing_matrix(partner_mesons[1], gamma_order[1], gamma_phase[1]),
        )
        for offset, (_, partner_mesons) in received.items()
    }
    centre_slices, partner_tiles = lax.optimization_barrier(
        (centre_slices, {offset: tile for offset, (tile, _) in received.items()})
    )
    for offset, tile in partner_tiles.items():
        source_partner, sink_partner = partner_weights[offset]
        forwards += [own_forward[offset], dress(source_partner, tile)]
        partners += [dress(sink_partner, tile), own_backward[offset]]
    rest = rest_loops(forwards, partners, shares)
    rest_slices = lax.all_to_all(rest, "src", split_axis=0, concat_axis=0, tiled=True)
    slices = jnp.concatenate([centre_slices, rest_slices], axis=1)
    block_count = slices.shape[0] * slices.shape[1]
    real_flat = slices[:, :, 0].reshape(block_count, -1)
    imag_flat = slices[:, :, 1].reshape(block_count, -1)
    trace_table = jnp.stack(
        [
            inner_product(real_flat, real_flat) - inner_product(imag_flat, imag_flat),
            inner_product(real_flat, imag_flat) + inner_product(imag_flat, real_flat),
        ]
    )
    place = np.zeros(block_count, np.int32)
    for source in range(shares):
        place[source * window + half_window] = source * window
        for offset in range(1, half_window + 1):
            place[source * window + half_window + offset] = source * window + 2 * offset - 1
            place[((source + offset) % shares) * window + half_window - offset] = source * window + 2 * offset
    canonical = jnp.asarray(place)
    trace_table = trace_table[:, canonical][:, :, canonical]
    summed = all_sum(trace_table, "src")
    return select_diagrams(summed, diagram_blocks, diagram_codes)


def solution(mesh):
    placed = (
        P(("groups", "src"), None, None, None, None),
        P(("groups", "src"), None, None, None),
        P(("groups", "src"), None, None, None),
        P(),
        P(),
        P(None, "src"),
        P("src"),
    )
    return jax.shard_map(
        per_device,
        mesh=mesh,
        in_specs=placed,
        out_specs=P(None, ("groups", "src")),
        check_vma=False,
    )
```

```python
import jax
import numpy as np
import jax.numpy as jnp
from jax import lax
from jax.experimental import pallas as pl
from jax.experimental.pallas import tpu as pltpu
from jax.sharding import PartitionSpec as P


def shifted(block, axis, distance):
    devices = range(lax.axis_size(axis))
    route = [((i - distance) % len(devices), i) for i in devices]
    return lax.ppermute(block, axis, route)


def gamma_parts(order_row, phase_row):
    spins = order_row.shape[0]
    chosen = (order_row[:, None] == jnp.arange(spins, dtype=jnp.int32)[None, :]).astype(jnp.float32)
    cosine = ((phase_row == 0).astype(jnp.float32) - (phase_row == 2).astype(jnp.float32))[:, None] * chosen
    sine = ((phase_row == 1).astype(jnp.float32) - (phase_row == 3).astype(jnp.float32))[:, None] * chosen
    return cosine, sine


def dressing_matrix(elemental, order_row, phase_row):
    cosine, sine = gamma_parts(order_row, phase_row)
    meson = elemental.astype(jnp.float32)
    kron_re = jnp.kron(cosine, meson[0]) - jnp.kron(sine, meson[1])
    kron_im = jnp.kron(cosine, meson[1]) + jnp.kron(sine, meson[0])
    top = jnp.concatenate([kron_re, -kron_im], axis=1)
    bottom = jnp.concatenate([kron_im, kron_re], axis=1)
    return jnp.concatenate([top, bottom], axis=0).astype(jnp.bfloat16)


def dress(weights, tile_pair):
    order = tile_pair.shape[-1]
    stacked = tile_pair.reshape(2 * order, order)
    out = jnp.dot(weights, stacked, preferred_element_type=jnp.float32)
    return out.astype(jnp.bfloat16).reshape(2, order, order)


def loop_kernel(forward_ref, backward_ref, out_ref):
    fr = forward_ref[0, 0]
    fi = forward_ref[0, 1]
    br = backward_ref[0, 0]
    bi = backward_ref[0, 1]
    shares = out_ref.shape[0]
    rows = out_ref.shape[3]
    real = jnp.dot(fr, br, preferred_element_type=jnp.float32) - jnp.dot(fi, bi, preferred_element_type=jnp.float32)
    imag = jnp.dot(fr, bi, preferred_element_type=jnp.float32) + jnp.dot(fi, br, preferred_element_type=jnp.float32)
    out_ref[:, 0, 0] = real.astype(out_ref.dtype).reshape(shares, rows, real.shape[-1])
    out_ref[:, 0, 1] = imag.astype(out_ref.dtype).reshape(shares, rows, imag.shape[-1])


def open_loops(forward, backward, shares):
    window, _, order, _ = forward.shape
    rows = order // shares
    tile = pl.BlockSpec((1, 2, order, order), lambda s: (s, 0, 0, 0))
    return pl.pallas_call(
        loop_kernel,
        grid=(window,),
        in_specs=[tile, tile],
        out_specs=pl.BlockSpec((shares, 1, 2, rows, order), lambda s: (0, s, 0, 0, 0)),
        out_shape=jax.ShapeDtypeStruct((shares, window, 2, rows, order), jnp.bfloat16),
        compiler_params=pltpu.CompilerParams(vmem_limit_bytes=48 * 1024 * 1024),
        cost_estimate=pl.CostEstimate(
            flops=8 * window * order ** 3, transcendentals=0, bytes_accessed=6 * window * order * order * 2
        ),
    )(forward, backward)


def rest_loop_kernel(*refs):
    count = (len(refs) - 1) // 2
    forward_refs, partner_refs, out_ref = refs[:count], refs[count:-1], refs[-1]
    step = pl.program_id(0)
    for index in range(count):

        @pl.when(step == index)
        def _():
            loop_kernel(forward_refs[index], partner_refs[index], out_ref)


def rest_loops(forwards, partners, shares):
    count = len(forwards)
    _, order, _ = forwards[0].shape
    rows = order // shares
    whole = pl.BlockSpec((1, 2, order, order), lambda s: (0, 0, 0, 0))
    return pl.pallas_call(
        rest_loop_kernel,
        grid=(count,),
        in_specs=[whole] * (2 * count),
        out_specs=pl.BlockSpec((shares, 1, 2, rows, order), lambda s: (0, s, 0, 0, 0)),
        out_shape=jax.ShapeDtypeStruct((shares, count, 2, rows, order), jnp.bfloat16),
        compiler_params=pltpu.CompilerParams(vmem_limit_bytes=56 * 1024 * 1024),
        cost_estimate=pl.CostEstimate(
            flops=8 * count * order ** 3, transcendentals=0, bytes_accessed=6 * count * order * order * 2
        ),
    )(*[tile[None] for tile in forwards], *[tile[None] for tile in partners])


def inner_product(left, right):
    return lax.dot_general(left, right, (((1,), (1,)), ((), ())), preferred_element_type=jnp.float32)


def all_sum(table, axis):
    n = lax.axis_size(axis)
    if n & (n - 1):
        return lax.psum(table, axis)
    bit = 1
    while bit < n:
        table = table + lax.ppermute(table, axis, [(i, i ^ bit) for i in range(n)])
        bit *= 2
    return table


def select_diagrams(trace_table, block_pairs, codes):
    signs = 1 - 2 * (codes % 2)
    scales = 1 + codes // 2
    weight = (signs * scales).astype(jnp.float32)
    return trace_table[:, block_pairs[0], block_pairs[1]] * weight[None, :]


def per_device(
    perambulator, source_meson, sink_meson, gamma_order, gamma_phase, diagram_blocks, diagram_codes
):
    window = perambulator.shape[1]
    half_window = window // 2
    shares = lax.axis_size("src")
    tiles = perambulator[0]
    mesons = jnp.stack([source_meson[0], sink_meson[0]])
    received = {}
    for offset in range(1, half_window + 1):
        received[offset] = (
            shifted(tiles[half_window - offset], "src", -offset),
            shifted(mesons, "src", -offset),
        )
    source_own = dressing_matrix(mesons[0], gamma_order[0], gamma_phase[0])
    sink_own = dressing_matrix(mesons[1], gamma_order[1], gamma_phase[1])
    forwards = [dress(source_own, tiles[half_window])]
    partners = [dress(sink_own, tiles[half_window])]
    for offset, (tile, partner_mesons) in received.items():
        source_partner = dressing_matrix(partner_mesons[0], gamma_order[0], gamma_phase[0])
        sink_partner = dressing_matrix(partner_mesons[1], gamma_order[1], gamma_phase[1])
        forwards += [dress(source_own, tiles[half_window + offset]), dress(source_partner, tile)]
        partners += [dress(sink_partner, tile), dress(sink_own, tiles[half_window + offset])]
    loops = rest_loops(forwards, partners, shares)
    slices = lax.all_to_all(loops, "src", split_axis=0, concat_axis=0, tiled=True)
    block_count = slices.shape[0] * slices.shape[1]
    real_flat = slices[:, :, 0].reshape(block_count, -1)
    imag_flat = slices[:, :, 1].reshape(block_count, -1)
    trace_table = jnp.stack(
        [
            inner_product(real_flat, real_flat) - inner_product(imag_flat, imag_flat),
            inner_product(real_flat, imag_flat) + inner_product(imag_flat, real_flat),
        ]
    )
    place = np.zeros(block_count, np.int32)
    for source in range(shares):
        place[source * window + half_window] = source * window
        for offset in range(1, half_window + 1):
            place[source * window + half_window + offset] = source * window + 2 * offset - 1
            place[((source + offset) % shares) * window + half_window - offset] = source * window + 2 * offset
    canonical = jnp.asarray(place)
    trace_table = trace_table[:, canonical][:, :, canonical]
    summed = all_sum(trace_table, "src")
    return select_diagrams(summed, diagram_blocks, diagram_codes)


def solution(mesh):
    placed = (
        P(("groups", "src"), None, None, None, None),
        P(("groups", "src"), None, None, None),
        P(("groups", "src"), None, None, None),
        P(),
        P(),
        P(None, "src"),
        P("src"),
    )
    return jax.shard_map(
        per_device,
        mesh=mesh,
        in_specs=placed,
        out_specs=P(None, ("groups", "src")),
        check_vma=False,
    )
```

```python
import jax
import numpy as np
import jax.numpy as jnp
from jax import lax
from jax.experimental import pallas as pl
from jax.experimental.pallas import tpu as pltpu
from jax.sharding import PartitionSpec as P


def shifted(block, axis, distance):
    devices = range(lax.axis_size(axis))
    route = [((i - distance) % len(devices), i) for i in devices]
    return lax.ppermute(block, axis, route)


def gamma_parts(order_row, phase_row):
    spins = order_row.shape[0]
    chosen = (order_row[:, None] == jnp.arange(spins, dtype=jnp.int32)[None, :]).astype(jnp.float32)
    cosine = ((phase_row == 0).astype(jnp.float32) - (phase_row == 2).astype(jnp.float32))[:, None] * chosen
    sine = ((phase_row == 1).astype(jnp.float32) - (phase_row == 3).astype(jnp.float32))[:, None] * chosen
    return cosine, sine


def dressing_matrix(elemental, order_row, phase_row):
    cosine, sine = gamma_parts(order_row, phase_row)
    meson = elemental.astype(jnp.float32)
    kron_re = jnp.kron(cosine, meson[0]) - jnp.kron(sine, meson[1])
    kron_im = jnp.kron(cosine, meson[1]) + jnp.kron(sine, meson[0])
    top = jnp.concatenate([kron_re, -kron_im], axis=1)
    bottom = jnp.concatenate([kron_im, kron_re], axis=1)
    return jnp.concatenate([top, bottom], axis=0).astype(jnp.bfloat16)


def dress(weights, tile_pair):
    order = tile_pair.shape[-1]
    stacked = tile_pair.reshape(2 * order, order)
    out = jnp.dot(weights, stacked, preferred_element_type=jnp.float32)
    return out.astype(jnp.bfloat16).reshape(2, order, order)


def loop_kernel(forward_ref, backward_ref, out_ref):
    fr = forward_ref[0, 0]
    fi = forward_ref[0, 1]
    br = backward_ref[0, 0]
    bi = backward_ref[0, 1]
    shares = out_ref.shape[0]
    rows = out_ref.shape[3]
    real = jnp.dot(fr, br, preferred_element_type=jnp.float32) - jnp.dot(fi, bi, preferred_element_type=jnp.float32)
    imag = jnp.dot(fr, bi, preferred_element_type=jnp.float32) + jnp.dot(fi, br, preferred_element_type=jnp.float32)
    out_ref[:, 0, 0] = real.astype(out_ref.dtype).reshape(shares, rows, real.shape[-1])
    out_ref[:, 0, 1] = imag.astype(out_ref.dtype).reshape(shares, rows, imag.shape[-1])


def open_loops(forward, backward, shares):
    window, _, order, _ = forward.shape
    rows = order // shares
    tile = pl.BlockSpec((1, 2, order, order), lambda s: (s, 0, 0, 0))
    return pl.pallas_call(
        loop_kernel,
        grid=(window,),
        in_specs=[tile, tile],
        out_specs=pl.BlockSpec((shares, 1, 2, rows, order), lambda s: (0, s, 0, 0, 0)),
        out_shape=jax.ShapeDtypeStruct((shares, window, 2, rows, order), jnp.bfloat16),
        compiler_params=pltpu.CompilerParams(vmem_limit_bytes=48 * 1024 * 1024),
        cost_estimate=pl.CostEstimate(
            flops=8 * window * order ** 3, transcendentals=0, bytes_accessed=6 * window * order * order * 2
        ),
    )(forward, backward)


def rest_loop_kernel(*refs):
    count = (len(refs) - 1) // 2
    forward_refs, partner_refs, out_ref = refs[:count], refs[count:-1], refs[-1]
    step = pl.program_id(0)
    for index in range(count):

        @pl.when(step == index)
        def _():
            loop_kernel(forward_refs[index], partner_refs[index], out_ref)


def rest_loops(forwards, partners, shares):
    count = len(forwards)
    _, order, _ = forwards[0].shape
    rows = order // shares
    whole = pl.BlockSpec((1, 2, order, order), lambda s: (0, 0, 0, 0))
    return pl.pallas_call(
        rest_loop_kernel,
        grid=(count,),
        in_specs=[whole] * (2 * count),
        out_specs=pl.BlockSpec((shares, 1, 2, rows, order), lambda s: (0, s, 0, 0, 0)),
        out_shape=jax.ShapeDtypeStruct((shares, count, 2, rows, order), jnp.bfloat16),
        compiler_params=pltpu.CompilerParams(vmem_limit_bytes=56 * 1024 * 1024),
        cost_estimate=pl.CostEstimate(
            flops=8 * count * order ** 3, transcendentals=0, bytes_accessed=6 * count * order * order * 2
        ),
    )(*[tile[None] for tile in forwards], *[tile[None] for tile in partners])


def inner_product(left, right):
    return lax.dot_general(left, right, (((1,), (1,)), ((), ())), preferred_element_type=jnp.float32)


def all_sum(table, axis):
    n = lax.axis_size(axis)
    if n & (n - 1):
        return lax.psum(table, axis)
    bit = 1
    while bit < n:
        table = table + lax.ppermute(table, axis, [(i, i ^ bit) for i in range(n)])
        bit *= 2
    return table


def select_diagrams(trace_table, block_pairs, codes):
    signs = 1 - 2 * (codes % 2)
    scales = 1 + codes // 2
    weight = (signs * scales).astype(jnp.float32)
    return trace_table[:, block_pairs[0], block_pairs[1]] * weight[None, :]


def per_device(
    perambulator, source_meson, sink_meson, gamma_order, gamma_phase, diagram_blocks, diagram_codes
):
    window = perambulator.shape[1]
    half_window = window // 2
    shares = lax.axis_size("src")
    tiles = perambulator[0]
    mesons = jnp.stack([source_meson[0], sink_meson[0]])
    received = {}
    for offset in range(1, half_window + 1):
        received[offset] = (
            shifted(tiles[half_window - offset], "src", -offset),
            shifted(mesons, "src", -offset),
        )
    source_own = dressing_matrix(mesons[0], gamma_order[0], gamma_phase[0])
    sink_own = dressing_matrix(mesons[1], gamma_order[1], gamma_phase[1])
    forwards = [dress(source_own, tiles[half_window])]
    partners = [dress(sink_own, tiles[half_window])]
    for offset, (tile, partner_mesons) in received.items():
        source_partner = dressing_matrix(partner_mesons[0], gamma_order[0], gamma_phase[0])
        sink_partner = dressing_matrix(partner_mesons[1], gamma_order[1], gamma_phase[1])
        forwards += [dress(source_own, tiles[half_window + offset]), dress(source_partner, tile)]
        partners += [dress(sink_partner, tile), dress(sink_own, tiles[half_window + offset])]
    loops = rest_loops(forwards, partners, shares)
    slices = lax.all_to_all(loops, "src", split_axis=0, concat_axis=0, tiled=True)
    sources, slots, _, rows, order = slices.shape
    block_count = sources * slots
    pieces = slices.reshape(2 * block_count, rows, order)
    grams = lax.dot_general(pieces, pieces, (((1, 2), (1, 2)), ((), ())), preferred_element_type=jnp.float32)
    grams = grams.reshape(block_count, 2, block_count, 2)
    trace_table = jnp.stack(
        [grams[:, 0, :, 0] - grams[:, 1, :, 1], grams[:, 0, :, 1] + grams[:, 1, :, 0]]
    )
    canonical_of_row = np.zeros(block_count, np.int32)
    for source in range(sources):
        canonical_of_row[source * window] = source * window + half_window
        for offset in range(1, half_window + 1):
            canonical_of_row[source * window + 2 * offset - 1] = source * window + half_window + offset
            canonical_of_row[source * window + 2 * offset] = ((source + offset) % sources) * window + half_window - offset
    row_of_canonical = jnp.asarray(np.argsort(canonical_of_row).astype(np.int32))
    trace_table = trace_table[:, row_of_canonical][:, :, row_of_canonical]
    summed = all_sum(trace_table, "src")
    return select_diagrams(summed, diagram_blocks, diagram_codes)


def select_rows(trace_table, canonical_of_row, block_pairs, codes):
    signs = 1 - 2 * (codes % 2)
    scales = 1 + codes // 2
    weight = (signs * scales).astype(jnp.float32)
    first = (block_pairs[0][:, None] == canonical_of_row[None, :]).astype(jnp.float32)
    second = (block_pairs[1][:, None] == canonical_of_row[None, :]).astype(jnp.float32)
    picked = jnp.einsum("dp,cpq->cdq", first, trace_table, precision=lax.Precision.HIGHEST)
    return jnp.sum(picked * second[None], axis=-1) * weight[None, :]


def solution(mesh):
    placed = (
        P(("groups", "src"), None, None, None, None),
        P(("groups", "src"), None, None, None),
        P(("groups", "src"), None, None, None),
        P(),
        P(),
        P(None, "src"),
        P("src"),
    )
    return jax.shard_map(
        per_device,
        mesh=mesh,
        in_specs=placed,
        out_specs=P(None, ("groups", "src")),
        check_vma=False,
    )
```

```python
import jax
import numpy as np
import jax.numpy as jnp
from jax import lax
from jax.experimental import pallas as pl
from jax.experimental.pallas import tpu as pltpu
from jax.sharding import PartitionSpec as P


def shifted(block, axis, distance):
    devices = range(lax.axis_size(axis))
    route = [((i - distance) % len(devices), i) for i in devices]
    return lax.ppermute(block, axis, route)


def gamma_parts(order_row, phase_row):
    spins = order_row.shape[0]
    chosen = (order_row[:, None] == jnp.arange(spins, dtype=jnp.int32)[None, :]).astype(jnp.float32)
    cosine = ((phase_row == 0).astype(jnp.float32) - (phase_row == 2).astype(jnp.float32))[:, None] * chosen
    sine = ((phase_row == 1).astype(jnp.float32) - (phase_row == 3).astype(jnp.float32))[:, None] * chosen
    return cosine, sine


def dressing_matrix(elemental, order_row, phase_row):
    cosine, sine = gamma_parts(order_row, phase_row)
    meson = elemental.astype(jnp.float32)
    kron_re = jnp.kron(cosine, meson[0]) - jnp.kron(sine, meson[1])
    kron_im = jnp.kron(cosine, meson[1]) + jnp.kron(sine, meson[0])
    top = jnp.concatenate([kron_re, -kron_im], axis=1)
    bottom = jnp.concatenate([kron_im, kron_re], axis=1)
    return jnp.concatenate([top, bottom], axis=0).astype(jnp.bfloat16)


def dress(weights, tile_pair):
    order = tile_pair.shape[-1]
    stacked = tile_pair.reshape(2 * order, order)
    out = jnp.dot(weights, stacked, preferred_element_type=jnp.float32)
    return out.astype(jnp.bfloat16).reshape(2, order, order)


def loop_kernel(forward_ref, backward_ref, out_ref):
    fr = forward_ref[0, 0]
    fi = forward_ref[0, 1]
    br = backward_ref[0, 0]
    bi = backward_ref[0, 1]
    shares = out_ref.shape[0]
    rows = out_ref.shape[3]
    real = jnp.dot(fr, br, preferred_element_type=jnp.float32) - jnp.dot(fi, bi, preferred_element_type=jnp.float32)
    imag = jnp.dot(fr, bi, preferred_element_type=jnp.float32) + jnp.dot(fi, br, preferred_element_type=jnp.float32)
    out_ref[:, 0, 0] = real.astype(out_ref.dtype).reshape(shares, rows, real.shape[-1])
    out_ref[:, 0, 1] = imag.astype(out_ref.dtype).reshape(shares, rows, imag.shape[-1])


def open_loops(forward, backward, shares):
    window, _, order, _ = forward.shape
    rows = order // shares
    tile = pl.BlockSpec((1, 2, order, order), lambda s: (s, 0, 0, 0))
    return pl.pallas_call(
        loop_kernel,
        grid=(window,),
        in_specs=[tile, tile],
        out_specs=pl.BlockSpec((shares, 1, 2, rows, order), lambda s: (0, s, 0, 0, 0)),
        out_shape=jax.ShapeDtypeStruct((shares, window, 2, rows, order), jnp.bfloat16),
        compiler_params=pltpu.CompilerParams(vmem_limit_bytes=48 * 1024 * 1024),
        cost_estimate=pl.CostEstimate(
            flops=8 * window * order ** 3, transcendentals=0, bytes_accessed=6 * window * order * order * 2
        ),
    )(forward, backward)


def rest_loop_kernel(*refs):
    count = (len(refs) - 1) // 2
    forward_refs, partner_refs, out_ref = refs[:count], refs[count:-1], refs[-1]
    step = pl.program_id(0)
    for index in range(count):

        @pl.when(step == index)
        def _():
            loop_kernel(forward_refs[index], partner_refs[index], out_ref)


def rest_loops(forwards, partners, shares):
    count = len(forwards)
    _, order, _ = forwards[0].shape
    rows = order // shares
    whole = pl.BlockSpec((1, 2, order, order), lambda s: (0, 0, 0, 0))
    return pl.pallas_call(
        rest_loop_kernel,
        grid=(count,),
        in_specs=[whole] * (2 * count),
        out_specs=pl.BlockSpec((shares, 1, 2, rows, order), lambda s: (0, s, 0, 0, 0)),
        out_shape=jax.ShapeDtypeStruct((shares, count, 2, rows, order), jnp.bfloat16),
        compiler_params=pltpu.CompilerParams(vmem_limit_bytes=56 * 1024 * 1024),
        cost_estimate=pl.CostEstimate(
            flops=8 * count * order ** 3, transcendentals=0, bytes_accessed=6 * count * order * order * 2
        ),
    )(*[tile[None] for tile in forwards], *[tile[None] for tile in partners])


def inner_product(left, right):
    return lax.dot_general(left, right, (((1,), (1,)), ((), ())), preferred_element_type=jnp.float32)


def all_sum(table, axis):
    n = lax.axis_size(axis)
    if n & (n - 1):
        return lax.psum(table, axis)
    bit = 1
    while bit < n:
        table = table + lax.ppermute(table, axis, [(i, i ^ bit) for i in range(n)])
        bit *= 2
    return table


def select_diagrams(trace_table, block_pairs, codes):
    signs = 1 - 2 * (codes % 2)
    scales = 1 + codes // 2
    weight = (signs * scales).astype(jnp.float32)
    blocks = jnp.arange(trace_table.shape[1], dtype=jnp.int32)
    first = (block_pairs[0][:, None] == blocks[None, :]).astype(jnp.float32)
    second = (block_pairs[1][:, None] == blocks[None, :]).astype(jnp.float32)
    picked = jnp.einsum("dp,cpq->cdq", first, trace_table, precision=lax.Precision.HIGHEST)
    return jnp.sum(picked * second[None], axis=-1) * weight[None, :]


def per_device(
    perambulator, source_meson, sink_meson, gamma_order, gamma_phase, diagram_blocks, diagram_codes
):
    window = perambulator.shape[1]
    half_window = window // 2
    shares = lax.axis_size("src")
    tiles = perambulator[0]
    mesons = jnp.stack([source_meson[0], sink_meson[0]])
    received = {}
    for offset in range(1, half_window + 1):
        received[offset] = (
            shifted(tiles[half_window - offset], "src", -offset),
            shifted(mesons, "src", -offset),
        )
    source_own = dressing_matrix(mesons[0], gamma_order[0], gamma_phase[0])
    sink_own = dressing_matrix(mesons[1], gamma_order[1], gamma_phase[1])
    forwards = [dress(source_own, tiles[half_window])]
    partners = [dress(sink_own, tiles[half_window])]
    for offset, (tile, partner_mesons) in received.items():
        source_partner = dressing_matrix(partner_mesons[0], gamma_order[0], gamma_phase[0])
        sink_partner = dressing_matrix(partner_mesons[1], gamma_order[1], gamma_phase[1])
        forwards += [dress(source_own, tiles[half_window + offset]), dress(source_partner, tile)]
        partners += [dress(sink_partner, tile), dress(sink_own, tiles[half_window + offset])]
    loops = rest_loops(forwards, partners, shares)
    slices = lax.all_to_all(loops, "src", split_axis=0, concat_axis=0, tiled=True)
    block_count = slices.shape[0] * slices.shape[1]
    real_flat = slices[:, :, 0].reshape(block_count, -1)
    imag_flat = slices[:, :, 1].reshape(block_count, -1)
    trace_table = jnp.stack(
        [
            inner_product(real_flat, real_flat) - inner_product(imag_flat, imag_flat),
            inner_product(real_flat, imag_flat) + inner_product(imag_flat, real_flat),
        ]
    )
    place = np.zeros(block_count, np.int32)
    for source in range(shares):
        place[source * window + half_window] = source * window
        for offset in range(1, half_window + 1):
            place[source * window + half_window + offset] = source * window + 2 * offset - 1
            place[((source + offset) % shares) * window + half_window - offset] = source * window + 2 * offset
    canonical = jnp.asarray(place)
    trace_table = trace_table[:, canonical][:, :, canonical]
    summed = all_sum(trace_table, "src")
    return select_diagrams(summed, diagram_blocks, diagram_codes)


def solution(mesh):
    placed = (
        P(("groups", "src"), None, None, None, None),
        P(("groups", "src"), None, None, None),
        P(("groups", "src"), None, None, None),
        P(),
        P(),
        P(None, "src"),
        P("src"),
    )
    return jax.shard_map(
        per_device,
        mesh=mesh,
        in_specs=placed,
        out_specs=P(None, ("groups", "src")),
        check_vma=False,
    )
```

```python
import jax
import numpy as np
import jax.numpy as jnp
from jax import lax
from jax.experimental import pallas as pl
from jax.experimental.pallas import tpu as pltpu
from jax.sharding import PartitionSpec as P


def shifted(block, axis, distance):
    devices = range(lax.axis_size(axis))
    route = [((i - distance) % len(devices), i) for i in devices]
    return lax.ppermute(block, axis, route)


def gamma_parts(order_row, phase_row):
    spins = order_row.shape[0]
    chosen = (order_row[:, None] == jnp.arange(spins, dtype=jnp.int32)[None, :]).astype(jnp.float32)
    cosine = ((phase_row == 0).astype(jnp.float32) - (phase_row == 2).astype(jnp.float32))[:, None] * chosen
    sine = ((phase_row == 1).astype(jnp.float32) - (phase_row == 3).astype(jnp.float32))[:, None] * chosen
    return cosine, sine


def dressing_matrix(elemental, order_row, phase_row):
    cosine, sine = gamma_parts(order_row, phase_row)
    meson = elemental.astype(jnp.float32)
    kron_re = jnp.kron(cosine, meson[0]) - jnp.kron(sine, meson[1])
    kron_im = jnp.kron(cosine, meson[1]) + jnp.kron(sine, meson[0])
    top = jnp.concatenate([kron_re, -kron_im], axis=1)
    bottom = jnp.concatenate([kron_im, kron_re], axis=1)
    return jnp.concatenate([top, bottom], axis=0).astype(jnp.bfloat16)


def dress(weights, tile_pair):
    order = tile_pair.shape[-1]
    stacked = tile_pair.reshape(2 * order, order)
    out = jnp.dot(weights, stacked, preferred_element_type=jnp.float32)
    return out.astype(jnp.bfloat16).reshape(2, order, order)


def loop_kernel(forward_ref, backward_ref, out_ref):
    fr = forward_ref[0, 0]
    fi = forward_ref[0, 1]
    br = backward_ref[0, 0]
    bi = backward_ref[0, 1]
    shares = out_ref.shape[0]
    rows = out_ref.shape[3]
    real = jnp.dot(fr, br, preferred_element_type=jnp.float32) - jnp.dot(fi, bi, preferred_element_type=jnp.float32)
    imag = jnp.dot(fr, bi, preferred_element_type=jnp.float32) + jnp.dot(fi, br, preferred_element_type=jnp.float32)
    out_ref[:, 0, 0] = real.astype(out_ref.dtype).reshape(shares, rows, real.shape[-1])
    out_ref[:, 1, 0] = imag.astype(out_ref.dtype).reshape(shares, rows, imag.shape[-1])


def rest_loop_kernel(*refs):
    count = (len(refs) - 1) // 2
    forward_refs, partner_refs, out_ref = refs[:count], refs[count:-1], refs[-1]
    step = pl.program_id(0)
    for index in range(count):

        @pl.when(step == index)
        def _():
            loop_kernel(forward_refs[index], partner_refs[index], out_ref)


def rest_loops(forwards, partners, shares):
    count = len(forwards)
    _, order, _ = forwards[0].shape
    rows = order // shares
    whole = pl.BlockSpec((1, 2, order, order), lambda s: (0, 0, 0, 0))
    return pl.pallas_call(
        rest_loop_kernel,
        grid=(count,),
        in_specs=[whole] * (2 * count),
        out_specs=pl.BlockSpec((shares, 2, 1, rows, order), lambda s: (0, 0, s, 0, 0)),
        out_shape=jax.ShapeDtypeStruct((shares, 2, count, rows, order), jnp.bfloat16),
        compiler_params=pltpu.CompilerParams(vmem_limit_bytes=56 * 1024 * 1024),
        cost_estimate=pl.CostEstimate(
            flops=8 * count * order ** 3, transcendentals=0, bytes_accessed=6 * count * order * order * 2
        ),
    )(*[tile[None] for tile in forwards], *[tile[None] for tile in partners])


def inner_product(left, right):
    return lax.dot_general(left, right, (((1,), (1,)), ((), ())), preferred_element_type=jnp.float32)


def all_sum(table, axis):
    n = lax.axis_size(axis)
    if n & (n - 1):
        return lax.psum(table, axis)
    bit = 1
    while bit < n:
        table = table + lax.ppermute(table, axis, [(i, i ^ bit) for i in range(n)])
        bit *= 2
    return table


def select_diagrams(trace_table, block_pairs, codes):
    signs = 1 - 2 * (codes % 2)
    scales = 1 + codes // 2
    weight = (signs * scales).astype(jnp.float32)
    blocks = jnp.arange(trace_table.shape[1], dtype=jnp.int32)
    first = (block_pairs[0][:, None] == blocks[None, :]).astype(jnp.float32)
    second = (block_pairs[1][:, None] == blocks[None, :]).astype(jnp.float32)
    picked = jnp.einsum("dp,cpq->cdq", first, trace_table, precision=lax.Precision.HIGHEST)
    return jnp.sum(picked * second[None], axis=-1) * weight[None, :]


def per_device(
    perambulator, source_meson, sink_meson, gamma_order, gamma_phase, diagram_blocks, diagram_codes
):
    window = perambulator.shape[1]
    half_window = window // 2
    shares = lax.axis_size("src")
    tiles = perambulator[0]
    mesons = jnp.stack([source_meson[0], sink_meson[0]])
    received = {}
    for offset in range(1, half_window + 1):
        received[offset] = (
            shifted(tiles[half_window - offset], "src", -offset),
            shifted(mesons, "src", -offset),
        )
    source_own = dressing_matrix(mesons[0], gamma_order[0], gamma_phase[0])
    sink_own = dressing_matrix(mesons[1], gamma_order[1], gamma_phase[1])
    forwards = [dress(source_own, tiles[half_window])]
    partners = [dress(sink_own, tiles[half_window])]
    for offset, (tile, partner_mesons) in received.items():
        source_partner = dressing_matrix(partner_mesons[0], gamma_order[0], gamma_phase[0])
        sink_partner = dressing_matrix(partner_mesons[1], gamma_order[1], gamma_phase[1])
        forwards += [dress(source_own, tiles[half_window + offset]), dress(source_partner, tile)]
        partners += [dress(sink_partner, tile), dress(sink_own, tiles[half_window + offset])]
    loops = rest_loops(forwards, partners, shares)
    slices = lax.all_to_all(loops, "src", split_axis=0, concat_axis=0, tiled=True)
    block_count = slices.shape[0] * slices.shape[2]
    real_flat = slices[:, 0].reshape(block_count, -1)
    imag_flat = slices[:, 1].reshape(block_count, -1)
    trace_table = jnp.stack(
        [
            inner_product(real_flat, real_flat) - inner_product(imag_flat, imag_flat),
            inner_product(real_flat, imag_flat) + inner_product(imag_flat, real_flat),
        ]
    )
    place = np.zeros(block_count, np.int32)
    for source in range(shares):
        place[source * window + half_window] = source * window
        for offset in range(1, half_window + 1):
            place[source * window + half_window + offset] = source * window + 2 * offset - 1
            place[((source + offset) % shares) * window + half_window - offset] = source * window + 2 * offset
    canonical = jnp.asarray(place)
    trace_table = trace_table[:, canonical][:, :, canonical]
    summed = all_sum(trace_table, "src")
    return select_diagrams(summed, diagram_blocks, diagram_codes)


def solution(mesh):
    placed = (
        P(("groups", "src"), None, None, None, None),
        P(("groups", "src"), None, None, None),
        P(("groups", "src"), None, None, None),
        P(),
        P(),
        P(None, "src"),
        P("src"),
    )
    return jax.shard_map(
        per_device,
        mesh=mesh,
        in_specs=placed,
        out_specs=P(None, ("groups", "src")),
        check_vma=False,
    )
```

```python
import jax
import numpy as np
import jax.numpy as jnp
from jax import lax
from jax.experimental import pallas as pl
from jax.experimental.pallas import tpu as pltpu
from jax.sharding import PartitionSpec as P


def shifted(block, axis, distance):
    devices = range(lax.axis_size(axis))
    route = [((i - distance) % len(devices), i) for i in devices]
    return lax.ppermute(block, axis, route)


def gamma_parts(order_row, phase_row):
    spins = order_row.shape[0]
    chosen = (order_row[:, None] == jnp.arange(spins, dtype=jnp.int32)[None, :]).astype(jnp.float32)
    cosine = ((phase_row == 0).astype(jnp.float32) - (phase_row == 2).astype(jnp.float32))[:, None] * chosen
    sine = ((phase_row == 1).astype(jnp.float32) - (phase_row == 3).astype(jnp.float32))[:, None] * chosen
    return cosine, sine


def dressing_matrix(elemental, order_row, phase_row):
    cosine, sine = gamma_parts(order_row, phase_row)
    meson = elemental.astype(jnp.float32)
    kron_re = jnp.kron(cosine, meson[0]) - jnp.kron(sine, meson[1])
    kron_im = jnp.kron(cosine, meson[1]) + jnp.kron(sine, meson[0])
    top = jnp.concatenate([kron_re, -kron_im], axis=1)
    bottom = jnp.concatenate([kron_im, kron_re], axis=1)
    return jnp.concatenate([top, bottom], axis=0).astype(jnp.bfloat16)


def dress(weights, tile_pair):
    order = tile_pair.shape[-1]
    stacked = tile_pair.reshape(2 * order, order)
    out = jnp.dot(weights, stacked, preferred_element_type=jnp.float32)
    return out.astype(jnp.bfloat16).reshape(2, order, order)


def dress_parts(weights, real, imag):
    order = real.shape[-1]
    out = jnp.dot(weights[:, :order], real, preferred_element_type=jnp.float32) + jnp.dot(
        weights[:, order:], imag, preferred_element_type=jnp.float32
    )
    return out.astype(jnp.bfloat16).reshape(2, order, order)


def loop_kernel(forward_ref, backward_ref, out_ref):
    fr = forward_ref[0, 0]
    fi = forward_ref[0, 1]
    br = backward_ref[0, 0]
    bi = backward_ref[0, 1]
    shares = out_ref.shape[0]
    rows = out_ref.shape[3]
    real = jnp.dot(fr, br, preferred_element_type=jnp.float32) - jnp.dot(fi, bi, preferred_element_type=jnp.float32)
    imag = jnp.dot(fr, bi, preferred_element_type=jnp.float32) + jnp.dot(fi, br, preferred_element_type=jnp.float32)
    out_ref[:, 0, 0] = real.astype(out_ref.dtype).reshape(shares, rows, real.shape[-1])
    out_ref[:, 1, 0] = imag.astype(out_ref.dtype).reshape(shares, rows, imag.shape[-1])


def rest_loop_kernel(*refs):
    count = (len(refs) - 1) // 2
    forward_refs, partner_refs, out_ref = refs[:count], refs[count:-1], refs[-1]
    step = pl.program_id(0)
    for index in range(count):

        @pl.when(step == index)
        def _():
            loop_kernel(forward_refs[index], partner_refs[index], out_ref)


def rest_loops(forwards, partners, shares):
    count = len(forwards)
    _, order, _ = forwards[0].shape
    rows = order // shares
    whole = pl.BlockSpec((1, 2, order, order), lambda s: (0, 0, 0, 0))
    return pl.pallas_call(
        rest_loop_kernel,
        grid=(count,),
        in_specs=[whole] * (2 * count),
        out_specs=pl.BlockSpec((shares, 2, 1, rows, order), lambda s: (0, 0, s, 0, 0)),
        out_shape=jax.ShapeDtypeStruct((shares, 2, count, rows, order), jnp.bfloat16),
        compiler_params=pltpu.CompilerParams(vmem_limit_bytes=56 * 1024 * 1024),
        cost_estimate=pl.CostEstimate(
            flops=8 * count * order ** 3, transcendentals=0, bytes_accessed=6 * count * order * order * 2
        ),
    )(*[tile[None] for tile in forwards], *[tile[None] for tile in partners])


def inner_product(left, right):
    return lax.dot_general(left, right, (((1,), (1,)), ((), ())), preferred_element_type=jnp.float32)


def all_sum(table, axis):
    n = lax.axis_size(axis)
    if n & (n - 1):
        return lax.psum(table, axis)
    bit = 1
    while bit < n:
        table = table + lax.ppermute(table, axis, [(i, i ^ bit) for i in range(n)])
        bit *= 2
    return table


def select_diagrams(trace_table, block_pairs, codes):
    signs = 1 - 2 * (codes % 2)
    scales = 1 + codes // 2
    weight = (signs * scales).astype(jnp.float32)
    blocks = jnp.arange(trace_table.shape[1], dtype=jnp.int32)
    first = (block_pairs[0][:, None] == blocks[None, :]).astype(jnp.float32)
    second = (block_pairs[1][:, None] == blocks[None, :]).astype(jnp.float32)
    picked = jnp.einsum("dp,cpq->cdq", first, trace_table, precision=lax.Precision.HIGHEST)
    return jnp.sum(picked * second[None], axis=-1) * weight[None, :]


def per_device(
    perambulator, source_meson, sink_meson, gamma_order, gamma_phase, diagram_blocks, diagram_codes
):
    window = perambulator.shape[1]
    half_window = window // 2
    shares = lax.axis_size("src")
    tiles = perambulator[0]
    mesons = jnp.stack([source_meson[0], sink_meson[0]])
    received = {}
    for offset in range(1, half_window + 1):
        received[offset] = (
            [shifted(tiles[half_window - offset, part], "src", -offset) for part in range(2)],
            shifted(mesons, "src", -offset),
        )
    source_own = dressing_matrix(mesons[0], gamma_order[0], gamma_phase[0])
    sink_own = dressing_matrix(mesons[1], gamma_order[1], gamma_phase[1])
    forwards = [dress(source_own, tiles[half_window])]
    partners = [dress(sink_own, tiles[half_window])]
    for offset, (tile, partner_mesons) in received.items():
        source_partner = dressing_matrix(partner_mesons[0], gamma_order[0], gamma_phase[0])
        sink_partner = dressing_matrix(partner_mesons[1], gamma_order[1], gamma_phase[1])
        forwards += [dress(source_own, tiles[half_window + offset]), dress_parts(source_partner, *tile)]
        partners += [dress_parts(sink_partner, *tile), dress(sink_own, tiles[half_window + offset])]
    loops = rest_loops(forwards, partners, shares)
    slices = lax.all_to_all(loops, "src", split_axis=0, concat_axis=0, tiled=True)
    block_count = slices.shape[0] * slices.shape[2]
    real_flat = slices[:, 0].reshape(block_count, -1)
    imag_flat = slices[:, 1].reshape(block_count, -1)
    trace_table = jnp.stack(
        [
            inner_product(real_flat, real_flat) - inner_product(imag_flat, imag_flat),
            inner_product(real_flat, imag_flat) + inner_product(imag_flat, real_flat),
        ]
    )
    place = np.zeros(block_count, np.int32)
    for source in range(shares):
        place[source * window + half_window] = source * window
        for offset in range(1, half_window + 1):
            place[source * window + half_window + offset] = source * window + 2 * offset - 1
            place[((source + offset) % shares) * window + half_window - offset] = source * window + 2 * offset
    canonical = jnp.asarray(place)
    trace_table = trace_table[:, canonical][:, :, canonical]
    summed = all_sum(trace_table, "src")
    return select_diagrams(summed, diagram_blocks, diagram_codes)


def solution(mesh):
    placed = (
        P(("groups", "src"), None, None, None, None),
        P(("groups", "src"), None, None, None),
        P(("groups", "src"), None, None, None),
        P(),
        P(),
        P(None, "src"),
        P("src"),
    )
    return jax.shard_map(
        per_device,
        mesh=mesh,
        in_specs=placed,
        out_specs=P(None, ("groups", "src")),
        check_vma=False,
    )
```

```python
import jax
import numpy as np
import jax.numpy as jnp
from jax import lax
from jax.experimental import pallas as pl
from jax.experimental.pallas import tpu as pltpu
from jax.sharding import PartitionSpec as P


def shifted(block, axis, distance):
    devices = range(lax.axis_size(axis))
    route = [((i - distance) % len(devices), i) for i in devices]
    return lax.ppermute(block, axis, route)


def gamma_parts(order_row, phase_row):
    spins = order_row.shape[0]
    chosen = (order_row[:, None] == jnp.arange(spins, dtype=jnp.int32)[None, :]).astype(jnp.float32)
    cosine = ((phase_row == 0).astype(jnp.float32) - (phase_row == 2).astype(jnp.float32))[:, None] * chosen
    sine = ((phase_row == 1).astype(jnp.float32) - (phase_row == 3).astype(jnp.float32))[:, None] * chosen
    return cosine, sine


def dressing_matrix(elemental, order_row, phase_row):
    cosine, sine = gamma_parts(order_row, phase_row)
    meson = elemental.astype(jnp.float32)
    kron_re = jnp.kron(cosine, meson[0]) - jnp.kron(sine, meson[1])
    kron_im = jnp.kron(cosine, meson[1]) + jnp.kron(sine, meson[0])
    top = jnp.concatenate([kron_re, -kron_im], axis=1)
    bottom = jnp.concatenate([kron_im, kron_re], axis=1)
    return jnp.concatenate([top, bottom], axis=0).astype(jnp.bfloat16)


def dress(weights, tile_pair):
    order = tile_pair.shape[-1]
    stacked = tile_pair.reshape(2 * order, order)
    out = jnp.dot(weights, stacked, preferred_element_type=jnp.float32)
    return out.astype(jnp.bfloat16).reshape(2, order, order)


def loop_kernel(forward_ref, backward_ref, out_ref):
    fr = forward_ref[0, 0]
    fi = forward_ref[0, 1]
    br = backward_ref[0, 0]
    bi = backward_ref[0, 1]
    shares = out_ref.shape[0]
    rows = out_ref.shape[3]
    joined = jnp.concatenate([fr, fi], axis=1)
    real = jnp.dot(joined, jnp.concatenate([br, -bi], axis=0), preferred_element_type=jnp.float32)
    imag = jnp.dot(joined, jnp.concatenate([bi, br], axis=0), preferred_element_type=jnp.float32)
    out_ref[:, 0, 0] = real.astype(out_ref.dtype).reshape(shares, rows, real.shape[-1])
    out_ref[:, 1, 0] = imag.astype(out_ref.dtype).reshape(shares, rows, imag.shape[-1])


def rest_loop_kernel(*refs):
    count = (len(refs) - 1) // 2
    forward_refs, partner_refs, out_ref = refs[:count], refs[count:-1], refs[-1]
    step = pl.program_id(0)
    for index in range(count):

        @pl.when(step == index)
        def _():
            loop_kernel(forward_refs[index], partner_refs[index], out_ref)


def rest_loops(forwards, partners, shares):
    count = len(forwards)
    _, order, _ = forwards[0].shape
    rows = order // shares
    whole = pl.BlockSpec((1, 2, order, order), lambda s: (0, 0, 0, 0))
    return pl.pallas_call(
        rest_loop_kernel,
        grid=(count,),
        in_specs=[whole] * (2 * count),
        out_specs=pl.BlockSpec((shares, 2, 1, rows, order), lambda s: (0, 0, s, 0, 0)),
        out_shape=jax.ShapeDtypeStruct((shares, 2, count, rows, order), jnp.bfloat16),
        compiler_params=pltpu.CompilerParams(vmem_limit_bytes=56 * 1024 * 1024),
        cost_estimate=pl.CostEstimate(
            flops=8 * count * order ** 3, transcendentals=0, bytes_accessed=6 * count * order * order * 2
        ),
    )(*[tile[None] for tile in forwards], *[tile[None] for tile in partners])


def inner_product(left, right):
    return lax.dot_general(left, right, (((1,), (1,)), ((), ())), preferred_element_type=jnp.float32)


def all_sum(table, axis):
    n = lax.axis_size(axis)
    if n & (n - 1):
        return lax.psum(table, axis)
    bit = 1
    while bit < n:
        table = table + lax.ppermute(table, axis, [(i, i ^ bit) for i in range(n)])
        bit *= 2
    return table


def select_diagrams(trace_table, block_pairs, codes):
    signs = 1 - 2 * (codes % 2)
    scales = 1 + codes // 2
    weight = (signs * scales).astype(jnp.float32)
    blocks = jnp.arange(trace_table.shape[1], dtype=jnp.int32)
    first = (block_pairs[0][:, None] == blocks[None, :]).astype(jnp.float32)
    second = (block_pairs[1][:, None] == blocks[None, :]).astype(jnp.float32)
    picked = jnp.einsum("dp,cpq->cdq", first, trace_table, precision=lax.Precision.HIGHEST)
    return jnp.sum(picked * second[None], axis=-1) * weight[None, :]


def per_device(
    perambulator, source_meson, sink_meson, gamma_order, gamma_phase, diagram_blocks, diagram_codes
):
    window = perambulator.shape[1]
    half_window = window // 2
    shares = lax.axis_size("src")
    tiles = perambulator[0]
    mesons = jnp.stack([source_meson[0], sink_meson[0]])
    received = {}
    for offset in range(1, half_window + 1):
        received[offset] = (
            shifted(tiles[half_window - offset], "src", -offset),
            shifted(mesons, "src", -offset),
        )
    source_own = dressing_matrix(mesons[0], gamma_order[0], gamma_phase[0])
    sink_own = dressing_matrix(mesons[1], gamma_order[1], gamma_phase[1])
    forwards = [dress(source_own, tiles[half_window])]
    partners = [dress(sink_own, tiles[half_window])]
    for offset, (tile, partner_mesons) in received.items():
        source_partner = dressing_matrix(partner_mesons[0], gamma_order[0], gamma_phase[0])
        sink_partner = dressing_matrix(partner_mesons[1], gamma_order[1], gamma_phase[1])
        forwards += [dress(source_own, tiles[half_window + offset]), dress(source_partner, tile)]
        partners += [dress(sink_partner, tile), dress(sink_own, tiles[half_window + offset])]
    loops = rest_loops(forwards, partners, shares)
    slices = lax.all_to_all(loops, "src", split_axis=0, concat_axis=0, tiled=True)
    block_count = slices.shape[0] * slices.shape[2]
    real_flat = slices[:, 0].reshape(block_count, -1)
    imag_flat = slices[:, 1].reshape(block_count, -1)
    trace_table = jnp.stack(
        [
            inner_product(real_flat, real_flat) - inner_product(imag_flat, imag_flat),
            inner_product(real_flat, imag_flat) + inner_product(imag_flat, real_flat),
        ]
    )
    place = np.zeros(block_count, np.int32)
    for source in range(shares):
        place[source * window + half_window] = source * window
        for offset in range(1, half_window + 1):
            place[source * window + half_window + offset] = source * window + 2 * offset - 1
            place[((source + offset) % shares) * window + half_window - offset] = source * window + 2 * offset
    canonical = jnp.asarray(place)
    trace_table = trace_table[:, canonical][:, :, canonical]
    summed = all_sum(trace_table, "src")
    return select_diagrams(summed, diagram_blocks, diagram_codes)


def solution(mesh):
    placed = (
        P(("groups", "src"), None, None, None, None),
        P(("groups", "src"), None, None, None),
        P(("groups", "src"), None, None, None),
        P(),
        P(),
        P(None, "src"),
        P("src"),
    )
    return jax.shard_map(
        per_device,
        mesh=mesh,
        in_specs=placed,
        out_specs=P(None, ("groups", "src")),
        check_vma=False,
    )
```

```python
import jax
import numpy as np
import jax.numpy as jnp
from jax import lax
from jax.experimental import pallas as pl
from jax.experimental.pallas import tpu as pltpu
from jax.sharding import PartitionSpec as P


def shifted(block, axis, distance):
    devices = range(lax.axis_size(axis))
    route = [((i - distance) % len(devices), i) for i in devices]
    return lax.ppermute(block, axis, route)


def gamma_parts(order_row, phase_row):
    spins = order_row.shape[0]
    chosen = (order_row[:, None] == jnp.arange(spins, dtype=jnp.int32)[None, :]).astype(jnp.float32)
    cosine = ((phase_row == 0).astype(jnp.float32) - (phase_row == 2).astype(jnp.float32))[:, None] * chosen
    sine = ((phase_row == 1).astype(jnp.float32) - (phase_row == 3).astype(jnp.float32))[:, None] * chosen
    return cosine, sine


def dressing_matrix(elemental, order_row, phase_row):
    cosine, sine = gamma_parts(order_row, phase_row)
    meson = elemental.astype(jnp.float32)
    kron_re = jnp.kron(cosine, meson[0]) - jnp.kron(sine, meson[1])
    kron_im = jnp.kron(cosine, meson[1]) + jnp.kron(sine, meson[0])
    top = jnp.concatenate([kron_re, -kron_im], axis=1)
    bottom = jnp.concatenate([kron_im, kron_re], axis=1)
    return jnp.concatenate([top, bottom], axis=0).astype(jnp.bfloat16)


def dress(weights, tile_pair):
    order = tile_pair.shape[-1]
    stacked = tile_pair.reshape(2 * order, order)
    out = jnp.dot(weights, stacked, preferred_element_type=jnp.float32)
    return out.astype(jnp.bfloat16).reshape(2, order, order)


def loop_body(fr, fi, br, bi, out_ref):
    shares = out_ref.shape[0]
    rows = out_ref.shape[3]
    joined = jnp.concatenate([fr, fi], axis=1)
    real = jnp.dot(joined, jnp.concatenate([br, -bi], axis=0), preferred_element_type=jnp.float32)
    imag = jnp.dot(joined, jnp.concatenate([bi, br], axis=0), preferred_element_type=jnp.float32)
    out_ref[:, 0, 0] = real.astype(out_ref.dtype).reshape(shares, rows, real.shape[-1])
    out_ref[:, 1, 0] = imag.astype(out_ref.dtype).reshape(shares, rows, imag.shape[-1])


def rest_loop_kernel(*refs):
    count = (len(refs) - 4) // 2
    forward_hbm, partner_hbm = refs[:count], refs[count : 2 * count]
    out_ref, forward_buf, partner_buf, sems = refs[2 * count :]
    step = pl.program_id(0)

    def copies(index):
        return (
            pltpu.make_async_copy(forward_hbm[index], forward_buf.at[index], sems.at[0, index]),
            pltpu.make_async_copy(partner_hbm[index], partner_buf.at[index], sems.at[1, index]),
        )

    @pl.when(step == 0)
    def _():
        for index in range(count):
            for copy in copies(index):
                copy.start()

    for index in range(count):

        @pl.when(step == index)
        def _():
            for copy in copies(index):
                copy.wait()
            loop_body(
                forward_buf[index, 0], forward_buf[index, 1], partner_buf[index, 0], partner_buf[index, 1], out_ref
            )


def rest_loops(forwards, partners, shares):
    count = len(forwards)
    _, order, _ = forwards[0].shape
    rows = order // shares
    return pl.pallas_call(
        rest_loop_kernel,
        grid=(count,),
        in_specs=[pl.BlockSpec(memory_space=pl.ANY)] * (2 * count),
        out_specs=pl.BlockSpec((shares, 2, 1, rows, order), lambda s: (0, 0, s, 0, 0)),
        out_shape=jax.ShapeDtypeStruct((shares, 2, count, rows, order), jnp.bfloat16),
        scratch_shapes=[
            pltpu.VMEM((count, 2, order, order), jnp.bfloat16),
            pltpu.VMEM((count, 2, order, order), jnp.bfloat16),
            pltpu.SemaphoreType.DMA((2, count)),
        ],
        compiler_params=pltpu.CompilerParams(vmem_limit_bytes=56 * 1024 * 1024),
        cost_estimate=pl.CostEstimate(
            flops=8 * count * order ** 3, transcendentals=0, bytes_accessed=6 * count * order * order * 2
        ),
    )(*forwards, *partners)


def inner_product(left, right):
    return lax.dot_general(left, right, (((1,), (1,)), ((), ())), preferred_element_type=jnp.float32)


def all_sum(table, axis):
    n = lax.axis_size(axis)
    if n & (n - 1):
        return lax.psum(table, axis)
    bit = 1
    while bit < n:
        table = table + lax.ppermute(table, axis, [(i, i ^ bit) for i in range(n)])
        bit *= 2
    return table


def select_diagrams(trace_table, block_pairs, codes):
    signs = 1 - 2 * (codes % 2)
    scales = 1 + codes // 2
    weight = (signs * scales).astype(jnp.float32)
    blocks = jnp.arange(trace_table.shape[1], dtype=jnp.int32)
    first = (block_pairs[0][:, None] == blocks[None, :]).astype(jnp.float32)
    second = (block_pairs[1][:, None] == blocks[None, :]).astype(jnp.float32)
    picked = jnp.einsum("dp,cpq->cdq", first, trace_table, precision=lax.Precision.HIGHEST)
    return jnp.sum(picked * second[None], axis=-1) * weight[None, :]


def per_device(
    perambulator, source_meson, sink_meson, gamma_order, gamma_phase, diagram_blocks, diagram_codes
):
    window = perambulator.shape[1]
    half_window = window // 2
    shares = lax.axis_size("src")
    tiles = perambulator[0]
    mesons = jnp.stack([source_meson[0], sink_meson[0]])
    received = {}
    for offset in range(1, half_window + 1):
        received[offset] = (
            shifted(tiles[half_window - offset], "src", -offset),
            shifted(mesons, "src", -offset),
        )
    source_own = dressing_matrix(mesons[0], gamma_order[0], gamma_phase[0])
    sink_own = dressing_matrix(mesons[1], gamma_order[1], gamma_phase[1])
    forwards = [dress(source_own, tiles[half_window])]
    partners = [dress(sink_own, tiles[half_window])]
    for offset, (tile, partner_mesons) in received.items():
        source_partner = dressing_matrix(partner_mesons[0], gamma_order[0], gamma_phase[0])
        sink_partner = dressing_matrix(partner_mesons[1], gamma_order[1], gamma_phase[1])
        forwards += [dress(source_own, tiles[half_window + offset]), dress(source_partner, tile)]
        partners += [dress(sink_partner, tile), dress(sink_own, tiles[half_window + offset])]
    loops = rest_loops(forwards, partners, shares)
    slices = lax.all_to_all(loops, "src", split_axis=0, concat_axis=0, tiled=True)
    block_count = slices.shape[0] * slices.shape[2]
    real_flat = slices[:, 0].reshape(block_count, -1)
    imag_flat = slices[:, 1].reshape(block_count, -1)
    trace_table = jnp.stack(
        [
            inner_product(real_flat, real_flat) - inner_product(imag_flat, imag_flat),
            inner_product(real_flat, imag_flat) + inner_product(imag_flat, real_flat),
        ]
    )
    place = np.zeros(block_count, np.int32)
    for source in range(shares):
        place[source * window + half_window] = source * window
        for offset in range(1, half_window + 1):
            place[source * window + half_window + offset] = source * window + 2 * offset - 1
            place[((source + offset) % shares) * window + half_window - offset] = source * window + 2 * offset
    canonical = jnp.asarray(place)
    trace_table = trace_table[:, canonical][:, :, canonical]
    summed = all_sum(trace_table, "src")
    return select_diagrams(summed, diagram_blocks, diagram_codes)


def solution(mesh):
    placed = (
        P(("groups", "src"), None, None, None, None),
        P(("groups", "src"), None, None, None),
        P(("groups", "src"), None, None, None),
        P(),
        P(),
        P(None, "src"),
        P("src"),
    )
    return jax.shard_map(
        per_device,
        mesh=mesh,
        in_specs=placed,
        out_specs=P(None, ("groups", "src")),
        check_vma=False,
    )
```

```python
import jax
import numpy as np
import jax.numpy as jnp
from jax import lax
from jax.experimental import pallas as pl
from jax.experimental.pallas import tpu as pltpu
from jax.sharding import PartitionSpec as P


def shifted(block, axis, distance):
    devices = range(lax.axis_size(axis))
    route = [((i - distance) % len(devices), i) for i in devices]
    return lax.ppermute(block, axis, route)


def gamma_parts(order_row, phase_row):
    spins = order_row.shape[0]
    chosen = (order_row[:, None] == jnp.arange(spins, dtype=jnp.int32)[None, :]).astype(jnp.float32)
    cosine = ((phase_row == 0).astype(jnp.float32) - (phase_row == 2).astype(jnp.float32))[:, None] * chosen
    sine = ((phase_row == 1).astype(jnp.float32) - (phase_row == 3).astype(jnp.float32))[:, None] * chosen
    return cosine, sine


def dressing_matrix(elemental, order_row, phase_row):
    cosine, sine = gamma_parts(order_row, phase_row)
    meson = elemental.astype(jnp.float32)
    kron_re = jnp.kron(cosine, meson[0]) - jnp.kron(sine, meson[1])
    kron_im = jnp.kron(cosine, meson[1]) + jnp.kron(sine, meson[0])
    top = jnp.concatenate([kron_re, -kron_im], axis=1)
    bottom = jnp.concatenate([kron_im, kron_re], axis=1)
    return jnp.concatenate([top, bottom], axis=0).astype(jnp.bfloat16)


def dress(weights, tile_pair):
    order = tile_pair.shape[-1]
    stacked = tile_pair.reshape(2 * order, order)
    out = jnp.dot(weights, stacked, preferred_element_type=jnp.float32)
    return out.astype(jnp.bfloat16).reshape(2, order, order)


def loop_body(fr, fi, br, bi, out_refs):
    shares = out_refs[0].shape[0]
    rows = out_refs[0].shape[3]
    joined = jnp.concatenate([fr, fi], axis=1)
    real = jnp.dot(joined, jnp.concatenate([br, -bi], axis=0), preferred_element_type=jnp.float32)
    imag = jnp.dot(joined, jnp.concatenate([bi, br], axis=0), preferred_element_type=jnp.float32)
    real = real.astype(jnp.bfloat16).reshape(shares, len(out_refs), rows, real.shape[-1])
    imag = imag.astype(jnp.bfloat16).reshape(shares, len(out_refs), rows, imag.shape[-1])
    for half, out_ref in enumerate(out_refs):
        out_ref[:, 0, 0] = real[:, half]
        out_ref[:, 1, 0] = imag[:, half]


def rest_loop_kernel(*refs):
    count = (len(refs) - 5) // 2
    forward_hbm, partner_hbm = refs[:count], refs[count : 2 * count]
    out_refs, (forward_buf, partner_buf, sems) = refs[2 * count : 2 * count + 2], refs[2 * count + 2 :]
    step = pl.program_id(0)

    def copies(index):
        return (
            pltpu.make_async_copy(forward_hbm[index], forward_buf.at[index], sems.at[0, index]),
            pltpu.make_async_copy(partner_hbm[index], partner_buf.at[index], sems.at[1, index]),
        )

    @pl.when(step == 0)
    def _():
        for index in range(count):
            for copy in copies(index):
                copy.start()

    for index in range(count):

        @pl.when(step == index)
        def _():
            for copy in copies(index):
                copy.wait()
            loop_body(
                forward_buf[index, 0], forward_buf[index, 1], partner_buf[index, 0], partner_buf[index, 1], out_refs
            )


def rest_loops(forwards, partners, shares):
    count = len(forwards)
    _, order, _ = forwards[0].shape
    rows = order // shares // 2
    half = jax.ShapeDtypeStruct((shares, 2, count, rows, order), jnp.bfloat16)
    return pl.pallas_call(
        rest_loop_kernel,
        grid=(count,),
        in_specs=[pl.BlockSpec(memory_space=pl.ANY)] * (2 * count),
        out_specs=[pl.BlockSpec((shares, 2, 1, rows, order), lambda s: (0, 0, s, 0, 0))] * 2,
        out_shape=[half, half],
        scratch_shapes=[
            pltpu.VMEM((count, 2, order, order), jnp.bfloat16),
            pltpu.VMEM((count, 2, order, order), jnp.bfloat16),
            pltpu.SemaphoreType.DMA((2, count)),
        ],
        compiler_params=pltpu.CompilerParams(vmem_limit_bytes=56 * 1024 * 1024),
        cost_estimate=pl.CostEstimate(
            flops=8 * count * order ** 3, transcendentals=0, bytes_accessed=6 * count * order * order * 2
        ),
    )(*forwards, *partners)


def inner_product(left, right):
    return lax.dot_general(left, right, (((1,), (1,)), ((), ())), preferred_element_type=jnp.float32)


def all_sum(table, axis):
    n = lax.axis_size(axis)
    if n & (n - 1):
        return lax.psum(table, axis)
    bit = 1
    while bit < n:
        table = table + lax.ppermute(table, axis, [(i, i ^ bit) for i in range(n)])
        bit *= 2
    return table


def select_diagrams(trace_table, block_pairs, codes):
    signs = 1 - 2 * (codes % 2)
    scales = 1 + codes // 2
    weight = (signs * scales).astype(jnp.float32)
    blocks = jnp.arange(trace_table.shape[1], dtype=jnp.int32)
    first = (block_pairs[0][:, None] == blocks[None, :]).astype(jnp.float32)
    second = (block_pairs[1][:, None] == blocks[None, :]).astype(jnp.float32)
    picked = jnp.einsum("dp,cpq->cdq", first, trace_table, precision=lax.Precision.HIGHEST)
    return jnp.sum(picked * second[None], axis=-1) * weight[None, :]


def per_device(
    perambulator, source_meson, sink_meson, gamma_order, gamma_phase, diagram_blocks, diagram_codes
):
    window = perambulator.shape[1]
    half_window = window // 2
    shares = lax.axis_size("src")
    tiles = perambulator[0]
    mesons = jnp.stack([source_meson[0], sink_meson[0]])
    received = {}
    for offset in range(1, half_window + 1):
        received[offset] = (
            shifted(tiles[half_window - offset], "src", -offset),
            shifted(mesons, "src", -offset),
        )
    source_own = dressing_matrix(mesons[0], gamma_order[0], gamma_phase[0])
    sink_own = dressing_matrix(mesons[1], gamma_order[1], gamma_phase[1])
    forwards = [dress(source_own, tiles[half_window])]
    partners = [dress(sink_own, tiles[half_window])]
    for offset, (tile, partner_mesons) in received.items():
        source_partner = dressing_matrix(partner_mesons[0], gamma_order[0], gamma_phase[0])
        sink_partner = dressing_matrix(partner_mesons[1], gamma_order[1], gamma_phase[1])
        forwards += [dress(source_own, tiles[half_window + offset]), dress(source_partner, tile)]
        partners += [dress(sink_partner, tile), dress(sink_own, tiles[half_window + offset])]
    trace_table = 0
    for loops in rest_loops(forwards, partners, shares):
        slices = lax.all_to_all(loops, "src", split_axis=0, concat_axis=0, tiled=True)
        block_count = slices.shape[0] * slices.shape[2]
        real_flat = slices[:, 0].reshape(block_count, -1)
        imag_flat = slices[:, 1].reshape(block_count, -1)
        trace_table = trace_table + jnp.stack(
            [
                inner_product(real_flat, real_flat) - inner_product(imag_flat, imag_flat),
                inner_product(real_flat, imag_flat) + inner_product(imag_flat, real_flat),
            ]
        )
    place = np.zeros(block_count, np.int32)
    for source in range(shares):
        place[source * window + half_window] = source * window
        for offset in range(1, half_window + 1):
            place[source * window + half_window + offset] = source * window + 2 * offset - 1
            place[((source + offset) % shares) * window + half_window - offset] = source * window + 2 * offset
    canonical = jnp.asarray(place)
    trace_table = trace_table[:, canonical][:, :, canonical]
    summed = all_sum(trace_table, "src")
    return select_diagrams(summed, diagram_blocks, diagram_codes)


def solution(mesh):
    placed = (
        P(("groups", "src"), None, None, None, None),
        P(("groups", "src"), None, None, None),
        P(("groups", "src"), None, None, None),
        P(),
        P(),
        P(None, "src"),
        P("src"),
    )
    return jax.shard_map(
        per_device,
        mesh=mesh,
        in_specs=placed,
        out_specs=P(None, ("groups", "src")),
        check_vma=False,
    )
```

```python
import functools

import jax
import numpy as np
import jax.numpy as jnp
from jax import lax
from jax.experimental import pallas as pl
from jax.experimental.pallas import tpu as pltpu
from jax.sharding import PartitionSpec as P


def shifted(block, axis, distance):
    devices = range(lax.axis_size(axis))
    route = [((i - distance) % len(devices), i) for i in devices]
    return lax.ppermute(block, axis, route)


def gamma_parts(order_row, phase_row):
    spins = order_row.shape[0]
    chosen = (order_row[:, None] == jnp.arange(spins, dtype=jnp.int32)[None, :]).astype(jnp.float32)
    cosine = ((phase_row == 0).astype(jnp.float32) - (phase_row == 2).astype(jnp.float32))[:, None] * chosen
    sine = ((phase_row == 1).astype(jnp.float32) - (phase_row == 3).astype(jnp.float32))[:, None] * chosen
    return cosine, sine


def dressing_matrix(elemental, order_row, phase_row):
    cosine, sine = gamma_parts(order_row, phase_row)
    meson = elemental.astype(jnp.float32)
    kron_re = jnp.kron(cosine, meson[0]) - jnp.kron(sine, meson[1])
    kron_im = jnp.kron(cosine, meson[1]) + jnp.kron(sine, meson[0])
    top = jnp.concatenate([kron_re, -kron_im], axis=1)
    bottom = jnp.concatenate([kron_im, kron_re], axis=1)
    return jnp.concatenate([top, bottom], axis=0).astype(jnp.bfloat16)


def dress(weights, tile_pair):
    order = tile_pair.shape[-1]
    stacked = tile_pair.reshape(2 * order, order)
    out = jnp.dot(weights, stacked, preferred_element_type=jnp.float32)
    return out.astype(jnp.bfloat16).reshape(2, order, order)


def loop_body(fr, fi, br, bi, out_ref):
    shares = out_ref.shape[0]
    rows = out_ref.shape[3]
    joined = jnp.concatenate([fr, fi], axis=1)
    real = jnp.dot(joined, jnp.concatenate([br, -bi], axis=0), preferred_element_type=jnp.float32)
    imag = jnp.dot(joined, jnp.concatenate([bi, br], axis=0), preferred_element_type=jnp.float32)
    out_ref[:, 0, 0] = real.astype(out_ref.dtype).reshape(shares, rows, real.shape[-1])
    out_ref[:, 1, 0] = imag.astype(out_ref.dtype).reshape(shares, rows, imag.shape[-1])


def rest_loop_kernel(count, *refs):
    forward_hbm, partner_hbm = refs[:count], refs[count : 2 * count]
    out_ref, forward_buf, partner_buf, sems = refs[-4:]
    step = pl.program_id(0)

    def copies(index):
        return (
            pltpu.make_async_copy(forward_hbm[index], forward_buf.at[index], sems.at[0, index]),
            pltpu.make_async_copy(partner_hbm[index], partner_buf.at[index], sems.at[1, index]),
        )

    @pl.when(step == 0)
    def _():
        for index in range(count):
            for copy in copies(index):
                copy.start()

    for index in range(count):

        @pl.when(step == index)
        def _():
            for copy in copies(index):
                copy.wait()
            loop_body(
                forward_buf[index, 0], forward_buf[index, 1], partner_buf[index, 0], partner_buf[index, 1], out_ref
            )


def rest_loops(forwards, partners, shares, total, first_slot, into=None):
    count = len(forwards)
    _, order, _ = forwards[0].shape
    rows = order // shares
    operands = [*forwards, *partners] + ([] if into is None else [into])
    return pl.pallas_call(
        functools.partial(rest_loop_kernel, count),
        grid=(count,),
        in_specs=[pl.BlockSpec(memory_space=pl.ANY)] * len(operands),
        out_specs=pl.BlockSpec((shares, 2, 1, rows, order), lambda s: (0, 0, s + first_slot, 0, 0)),
        out_shape=jax.ShapeDtypeStruct((shares, 2, total, rows, order), jnp.bfloat16),
        scratch_shapes=[
            pltpu.VMEM((count, 2, order, order), jnp.bfloat16),
            pltpu.VMEM((count, 2, order, order), jnp.bfloat16),
            pltpu.SemaphoreType.DMA((2, count)),
        ],
        input_output_aliases={} if into is None else {2 * count: 0},
        compiler_params=pltpu.CompilerParams(vmem_limit_bytes=56 * 1024 * 1024),
        cost_estimate=pl.CostEstimate(
            flops=8 * count * order ** 3, transcendentals=0, bytes_accessed=6 * count * order * order * 2
        ),
    )(*operands)


def inner_product(left, right):
    return lax.dot_general(left, right, (((1,), (1,)), ((), ())), preferred_element_type=jnp.float32)


def all_sum(table, axis):
    n = lax.axis_size(axis)
    if n & (n - 1):
        return lax.psum(table, axis)
    bit = 1
    while bit < n:
        table = table + lax.ppermute(table, axis, [(i, i ^ bit) for i in range(n)])
        bit *= 2
    return table


def select_diagrams(trace_table, block_pairs, codes):
    signs = 1 - 2 * (codes % 2)
    scales = 1 + codes // 2
    weight = (signs * scales).astype(jnp.float32)
    blocks = jnp.arange(trace_table.shape[1], dtype=jnp.int32)
    first = (block_pairs[0][:, None] == blocks[None, :]).astype(jnp.float32)
    second = (block_pairs[1][:, None] == blocks[None, :]).astype(jnp.float32)
    picked = jnp.einsum("dp,cpq->cdq", first, trace_table, precision=lax.Precision.HIGHEST)
    return jnp.sum(picked * second[None], axis=-1) * weight[None, :]


def per_device(
    perambulator, source_meson, sink_meson, gamma_order, gamma_phase, diagram_blocks, diagram_codes
):
    window = perambulator.shape[1]
    half_window = window // 2
    shares = lax.axis_size("src")
    tiles = perambulator[0]
    mesons = jnp.stack([source_meson[0], sink_meson[0]])
    received = {}
    for offset in range(1, half_window + 1):
        received[offset] = (
            shifted(tiles[half_window - offset], "src", -offset),
            shifted(mesons, "src", -offset),
        )
    source_own = dressing_matrix(mesons[0], gamma_order[0], gamma_phase[0])
    sink_own = dressing_matrix(mesons[1], gamma_order[1], gamma_phase[1])
    forwards = [dress(source_own, tiles[half_window])]
    partners = [dress(sink_own, tiles[half_window])]
    for offset, (tile, partner_mesons) in received.items():
        source_partner = dressing_matrix(partner_mesons[0], gamma_order[0], gamma_phase[0])
        sink_partner = dressing_matrix(partner_mesons[1], gamma_order[1], gamma_phase[1])
        forwards += [dress(source_own, tiles[half_window + offset]), dress(source_partner, tile)]
        partners += [dress(sink_partner, tile), dress(sink_own, tiles[half_window + offset])]
    loops = rest_loops(forwards[:1], partners[:1], shares, window, 0)
    loops = rest_loops(forwards[1:], partners[1:], shares, window, 1, into=loops)
    slices = lax.all_to_all(loops, "src", split_axis=0, concat_axis=0, tiled=True)
    block_count = slices.shape[0] * slices.shape[2]
    real_flat = slices[:, 0].reshape(block_count, -1)
    imag_flat = slices[:, 1].reshape(block_count, -1)
    trace_table = jnp.stack(
        [
            inner_product(real_flat, real_flat) - inner_product(imag_flat, imag_flat),
            inner_product(real_flat, imag_flat) + inner_product(imag_flat, real_flat),
        ]
    )
    place = np.zeros(block_count, np.int32)
    for source in range(shares):
        place[source * window + half_window] = source * window
        for offset in range(1, half_window + 1):
            place[source * window + half_window + offset] = source * window + 2 * offset - 1
            place[((source + offset) % shares) * window + half_window - offset] = source * window + 2 * offset
    canonical = jnp.asarray(place)
    trace_table = trace_table[:, canonical][:, :, canonical]
    summed = all_sum(trace_table, "src")
    return select_diagrams(summed, diagram_blocks, diagram_codes)


def solution(mesh):
    placed = (
        P(("groups", "src"), None, None, None, None),
        P(("groups", "src"), None, None, None),
        P(("groups", "src"), None, None, None),
        P(),
        P(),
        P(None, "src"),
        P("src"),
    )
    return jax.shard_map(
        per_device,
        mesh=mesh,
        in_specs=placed,
        out_specs=P(None, ("groups", "src")),
        check_vma=False,
    )
```

```python
import jax
import numpy as np
import jax.numpy as jnp
from jax import lax
from jax.experimental import pallas as pl
from jax.experimental.pallas import tpu as pltpu
from jax.sharding import PartitionSpec as P


def shifted(block, axis, distance):
    devices = range(lax.axis_size(axis))
    route = [((i - distance) % len(devices), i) for i in devices]
    return lax.ppermute(block, axis, route)


def gamma_parts(order_row, phase_row):
    spins = order_row.shape[0]
    chosen = (order_row[:, None] == jnp.arange(spins, dtype=jnp.int32)[None, :]).astype(jnp.float32)
    cosine = ((phase_row == 0).astype(jnp.float32) - (phase_row == 2).astype(jnp.float32))[:, None] * chosen
    sine = ((phase_row == 1).astype(jnp.float32) - (phase_row == 3).astype(jnp.float32))[:, None] * chosen
    return cosine, sine


def dressing_matrix(elemental, order_row, phase_row):
    cosine, sine = gamma_parts(order_row, phase_row)
    meson = elemental.astype(jnp.float32)
    kron_re = jnp.kron(cosine, meson[0]) - jnp.kron(sine, meson[1])
    kron_im = jnp.kron(cosine, meson[1]) + jnp.kron(sine, meson[0])
    top = jnp.concatenate([kron_re, -kron_im], axis=1)
    bottom = jnp.concatenate([kron_im, kron_re], axis=1)
    return jnp.concatenate([top, bottom], axis=0).astype(jnp.bfloat16)


def dress(weights, tile_pair):
    order = tile_pair.shape[-1]
    stacked = tile_pair.reshape(2 * order, order)
    out = jnp.dot(weights, stacked, preferred_element_type=jnp.float32)
    return out.astype(jnp.bfloat16).reshape(2, order, order)


def loop_body(fr, fi, br, bi, out_ref):
    shares = out_ref.shape[0]
    rows = out_ref.shape[3]
    joined = jnp.concatenate([fr, fi], axis=1)
    real = jnp.dot(joined, jnp.concatenate([br, -bi], axis=0), preferred_element_type=jnp.float32)
    imag = jnp.dot(joined, jnp.concatenate([bi, br], axis=0), preferred_element_type=jnp.float32)
    out_ref[:, 0, 0] = real.astype(out_ref.dtype).reshape(shares, rows, real.shape[-1])
    out_ref[:, 1, 0] = imag.astype(out_ref.dtype).reshape(shares, rows, imag.shape[-1])


def rest_loop_kernel(*refs):
    count = (len(refs) - 4) // 2
    forward_hbm, partner_hbm = refs[:count], refs[count : 2 * count]
    out_ref, forward_buf, partner_buf, sems = refs[2 * count :]
    step = pl.program_id(0)

    def copies(index):
        return (
            pltpu.make_async_copy(forward_hbm[index], forward_buf.at[index], sems.at[0, index]),
            pltpu.make_async_copy(partner_hbm[index], partner_buf.at[index], sems.at[1, index]),
        )

    @pl.when(step == 0)
    def _():
        for index in range(count):
            for copy in copies(index):
                copy.start()

    for index in range(count):

        @pl.when(step == index)
        def _():
            for copy in copies(index):
                copy.wait()
            loop_body(
                forward_buf[index, 0], forward_buf[index, 1], partner_buf[index, 0], partner_buf[index, 1], out_ref
            )


def rest_loops(forwards, partners, shares):
    count = len(forwards)
    _, order, _ = forwards[0].shape
    rows = order // shares
    return pl.pallas_call(
        rest_loop_kernel,
        grid=(count,),
        in_specs=[pl.BlockSpec(memory_space=pl.ANY)] * (2 * count),
        out_specs=pl.BlockSpec((shares, 2, 1, rows, order), lambda s: (0, 0, s, 0, 0)),
        out_shape=jax.ShapeDtypeStruct((shares, 2, count, rows, order), jnp.bfloat16),
        scratch_shapes=[
            pltpu.VMEM((count, 2, order, order), jnp.bfloat16),
            pltpu.VMEM((count, 2, order, order), jnp.bfloat16),
            pltpu.SemaphoreType.DMA((2, count)),
        ],
        compiler_params=pltpu.CompilerParams(vmem_limit_bytes=56 * 1024 * 1024),
        cost_estimate=pl.CostEstimate(
            flops=8 * count * order ** 3, transcendentals=0, bytes_accessed=6 * count * order * order * 2
        ),
    )(*forwards, *partners)


def inner_product(left, right):
    return lax.dot_general(left, right, (((1,), (1,)), ((), ())), preferred_element_type=jnp.float32)


def all_sum(table, axis):
    n = lax.axis_size(axis)
    if n & (n - 1):
        return lax.psum(table, axis)
    bit = 1
    while bit < n:
        table = table + lax.ppermute(table, axis, [(i, i ^ bit) for i in range(n)])
        bit *= 2
    return table


def select_diagrams(trace_table, block_pairs, codes):
    signs = 1 - 2 * (codes % 2)
    scales = 1 + codes // 2
    weight = (signs * scales).astype(jnp.float32)
    blocks = jnp.arange(trace_table.shape[1], dtype=jnp.int32)
    first = (block_pairs[0][:, None] == blocks[None, :]).astype(jnp.float32)
    second = (block_pairs[1][:, None] == blocks[None, :]).astype(jnp.float32)
    picked = jnp.einsum("dp,cpq->cdq", first, trace_table, precision=lax.Precision.HIGHEST)
    return jnp.sum(picked * second[None], axis=-1) * weight[None, :]


def per_device(
    perambulator, source_meson, sink_meson, gamma_order, gamma_phase, diagram_blocks, diagram_codes
):
    window = perambulator.shape[1]
    half_window = window // 2
    shares = lax.axis_size("src")
    tiles = perambulator[0]
    mesons = jnp.stack([source_meson[0], sink_meson[0]])
    received = {}
    for offset in range(1, half_window + 1):
        received[offset] = (
            shifted(tiles[half_window - offset], "src", -offset),
            shifted(mesons, "src", -offset),
        )
    source_own = dressing_matrix(mesons[0], gamma_order[0], gamma_phase[0])
    sink_own = dressing_matrix(mesons[1], gamma_order[1], gamma_phase[1])
    forwards = [dress(source_own, tiles[half_window])]
    partners = [dress(sink_own, tiles[half_window])]
    for offset, (tile, partner_mesons) in received.items():
        source_partner = dressing_matrix(partner_mesons[0], gamma_order[0], gamma_phase[0])
        sink_partner = dressing_matrix(partner_mesons[1], gamma_order[1], gamma_phase[1])
        order = tile.shape[-1]
        both = jnp.dot(
            jnp.concatenate([source_partner, sink_partner], axis=0),
            tile.reshape(2 * order, order),
            preferred_element_type=jnp.float32,
        ).astype(jnp.bfloat16)
        forwards += [dress(source_own, tiles[half_window + offset]), both[: 2 * order].reshape(2, order, order)]
        partners += [both[2 * order :].reshape(2, order, order), dress(sink_own, tiles[half_window + offset])]
    loops = rest_loops(forwards, partners, shares)
    slices = lax.all_to_all(loops, "src", split_axis=0, concat_axis=0, tiled=True)
    block_count = slices.shape[0] * slices.shape[2]
    real_flat = slices[:, 0].reshape(block_count, -1)
    imag_flat = slices[:, 1].reshape(block_count, -1)
    trace_table = jnp.stack(
        [
            inner_product(real_flat, real_flat) - inner_product(imag_flat, imag_flat),
            inner_product(real_flat, imag_flat) + inner_product(imag_flat, real_flat),
        ]
    )
    place = np.zeros(block_count, np.int32)
    for source in range(shares):
        place[source * window + half_window] = source * window
        for offset in range(1, half_window + 1):
            place[source * window + half_window + offset] = source * window + 2 * offset - 1
            place[((source + offset) % shares) * window + half_window - offset] = source * window + 2 * offset
    canonical = jnp.asarray(place)
    trace_table = trace_table[:, canonical][:, :, canonical]
    summed = all_sum(trace_table, "src")
    return select_diagrams(summed, diagram_blocks, diagram_codes)


def solution(mesh):
    placed = (
        P(("groups", "src"), None, None, None, None),
        P(("groups", "src"), None, None, None),
        P(("groups", "src"), None, None, None),
        P(),
        P(),
        P(None, "src"),
        P("src"),
    )
    return jax.shard_map(
        per_device,
        mesh=mesh,
        in_specs=placed,
        out_specs=P(None, ("groups", "src")),
        check_vma=False,
    )
```

```python
import jax
import numpy as np
import jax.numpy as jnp
from jax import lax
from jax.experimental import pallas as pl
from jax.experimental.pallas import tpu as pltpu
from jax.sharding import PartitionSpec as P


def shifted(block, axis, distance):
    devices = range(lax.axis_size(axis))
    route = [((i - distance) % len(devices), i) for i in devices]
    return lax.ppermute(block, axis, route)


def gamma_parts(order_row, phase_row):
    spins = order_row.shape[0]
    chosen = (order_row[:, None] == jnp.arange(spins, dtype=jnp.int32)[None, :]).astype(jnp.float32)
    cosine = ((phase_row == 0).astype(jnp.float32) - (phase_row == 2).astype(jnp.float32))[:, None] * chosen
    sine = ((phase_row == 1).astype(jnp.float32) - (phase_row == 3).astype(jnp.float32))[:, None] * chosen
    return cosine, sine


def dressing_matrix(elemental, order_row, phase_row):
    cosine, sine = gamma_parts(order_row, phase_row)
    meson = elemental.astype(jnp.float32)
    kron_re = jnp.kron(cosine, meson[0]) - jnp.kron(sine, meson[1])
    kron_im = jnp.kron(cosine, meson[1]) + jnp.kron(sine, meson[0])
    top = jnp.concatenate([kron_re, -kron_im], axis=1)
    bottom = jnp.concatenate([kron_im, kron_re], axis=1)
    return jnp.concatenate([top, bottom], axis=0).astype(jnp.bfloat16)


def dress(weights, tile_pair):
    order = tile_pair.shape[-1]
    stacked = tile_pair.reshape(2 * order, order)
    out = jnp.dot(weights, stacked, preferred_element_type=jnp.float32)
    return out.astype(jnp.bfloat16).reshape(2, order, order)


def loop_body(fr, fi, br, bi, out_ref):
    shares = out_ref.shape[0]
    rows = out_ref.shape[3]
    joined = jnp.concatenate([fr, fi], axis=1)
    real = jnp.dot(joined, jnp.concatenate([br, -bi], axis=0), preferred_element_type=jnp.float32)
    imag = jnp.dot(joined, jnp.concatenate([bi, br], axis=0), preferred_element_type=jnp.float32)
    out_ref[:, 0, 0] = real.astype(out_ref.dtype).reshape(shares, rows, real.shape[-1])
    out_ref[:, 1, 0] = imag.astype(out_ref.dtype).reshape(shares, rows, imag.shape[-1])


def rest_loop_kernel(*refs):
    count = (len(refs) - 4) // 2
    forward_hbm, partner_hbm = refs[:count], refs[count : 2 * count]
    out_ref, forward_buf, partner_buf, sems = refs[2 * count :]
    step = pl.program_id(0)

    def copies(index):
        return (
            pltpu.make_async_copy(forward_hbm[index], forward_buf.at[index], sems.at[0, index]),
            pltpu.make_async_copy(partner_hbm[index], partner_buf.at[index], sems.at[1, index]),
        )

    @pl.when(step == 0)
    def _():
        for index in range(count):
            for copy in copies(index):
                copy.start()

    for index in range(count):

        @pl.when(step == index)
        def _():
            for copy in copies(index):
                copy.wait()
            loop_body(
                forward_buf[index, 0], forward_buf[index, 1], partner_buf[index, 0], partner_buf[index, 1], out_ref
            )


def rest_loops(forwards, partners, shares):
    count = len(forwards)
    _, order, _ = forwards[0].shape
    rows = order // shares
    return pl.pallas_call(
        rest_loop_kernel,
        grid=(count,),
        in_specs=[pl.BlockSpec(memory_space=pl.ANY)] * (2 * count),
        out_specs=pl.BlockSpec((shares, 2, 1, rows, order), lambda s: (0, 0, s, 0, 0)),
        out_shape=jax.ShapeDtypeStruct((shares, 2, count, rows, order), jnp.bfloat16),
        scratch_shapes=[
            pltpu.VMEM((count, 2, order, order), jnp.bfloat16),
            pltpu.VMEM((count, 2, order, order), jnp.bfloat16),
            pltpu.SemaphoreType.DMA((2, count)),
        ],
        compiler_params=pltpu.CompilerParams(vmem_limit_bytes=56 * 1024 * 1024),
        cost_estimate=pl.CostEstimate(
            flops=8 * count * order ** 3, transcendentals=0, bytes_accessed=6 * count * order * order * 2
        ),
    )(*forwards, *partners)


def inner_product(left, right):
    return lax.dot_general(left, right, (((1,), (1,)), ((), ())), preferred_element_type=jnp.float32)


def all_sum(table, axis):
    n = lax.axis_size(axis)
    if n & (n - 1):
        return lax.psum(table, axis)
    bit = 1
    while bit < n:
        table = table + lax.ppermute(table, axis, [(i, i ^ bit) for i in range(n)])
        bit *= 2
    return table


def select_diagrams(trace_table, block_pairs, codes):
    signs = 1 - 2 * (codes % 2)
    scales = 1 + codes // 2
    weight = (signs * scales).astype(jnp.float32)
    blocks = jnp.arange(trace_table.shape[1], dtype=jnp.int32)
    first = (block_pairs[0][:, None] == blocks[None, :]).astype(jnp.float32)
    second = (block_pairs[1][:, None] == blocks[None, :]).astype(jnp.float32)
    picked = jnp.einsum("dp,cpq->cdq", first, trace_table, precision=lax.Precision.HIGHEST)
    return jnp.sum(picked * second[None], axis=-1) * weight[None, :]


def per_device(
    perambulator, source_meson, sink_meson, gamma_order, gamma_phase, diagram_blocks, diagram_codes
):
    window = perambulator.shape[1]
    half_window = window // 2
    shares = lax.axis_size("src")
    tiles = perambulator[0]
    mesons = jnp.stack([source_meson[0], sink_meson[0]])
    received = {}
    for offset in range(1, half_window + 1):
        received[offset] = (
            shifted(tiles[half_window - offset], "src", -offset),
            shifted(mesons, "src", -offset),
        )
    source_own = dressing_matrix(mesons[0], gamma_order[0], gamma_phase[0])
    sink_own = dressing_matrix(mesons[1], gamma_order[1], gamma_phase[1])
    forwards = [dress(source_own, tiles[half_window])]
    partners = [dress(sink_own, tiles[half_window])]
    for offset, (tile, partner_mesons) in received.items():
        source_partner = dressing_matrix(partner_mesons[0], gamma_order[0], gamma_phase[0])
        sink_partner = dressing_matrix(partner_mesons[1], gamma_order[1], gamma_phase[1])
        forwards += [dress(source_own, tiles[half_window + offset]), dress(source_partner, tile)]
        partners += [dress(sink_partner, tile), dress(sink_own, tiles[half_window + offset])]
    loops = rest_loops(forwards, partners, shares)
    slices = lax.all_to_all(loops, "src", split_axis=0, concat_axis=0, tiled=True)
    block_count = slices.shape[0] * slices.shape[2]
    real_flat = slices[:, 0].reshape(block_count, -1)
    imag_flat = slices[:, 1].reshape(block_count, -1)
    mixed = inner_product(real_flat, imag_flat)
    trace_table = jnp.stack(
        [inner_product(real_flat, real_flat) - inner_product(imag_flat, imag_flat), mixed + mixed.T]
    )
    place = np.zeros(block_count, np.int32)
    for source in range(shares):
        place[source * window + half_window] = source * window
        for offset in range(1, half_window + 1):
            place[source * window + half_window + offset] = source * window + 2 * offset - 1
            place[((source + offset) % shares) * window + half_window - offset] = source * window + 2 * offset
    canonical = jnp.asarray(place)
    trace_table = trace_table[:, canonical][:, :, canonical]
    summed = all_sum(trace_table, "src")
    return select_diagrams(summed, diagram_blocks, diagram_codes)


def solution(mesh):
    placed = (
        P(("groups", "src"), None, None, None, None),
        P(("groups", "src"), None, None, None),
        P(("groups", "src"), None, None, None),
        P(),
        P(),
        P(None, "src"),
        P("src"),
    )
    return jax.shard_map(
        per_device,
        mesh=mesh,
        in_specs=placed,
        out_specs=P(None, ("groups", "src")),
        check_vma=False,
    )
```
